32 devices in a mesh: grp: 2 (over x), blade: 8 (over z, y), dof: 2 (over core).
Axes of the slice: x: 2, y: 2, z: 4, core: 2. Of those that a mesh axis runs over, the one named last changes fastest.
Arguments:
- panel: bfloat16 [8192, 512], P(('grp', 'blade', 'dof')), parts along dimension 0, may hold values from -0.25 to 0.25
- stiffness: bfloat16 [96, 64, 128, 128], P(('grp', 'blade'), 'dof'), parts along dimension 0, may hold values from -0.5 to 0.5
- block_rows: int32 [96, 64], P(('grp', 'blade'), 'dof'), parts along dimension 0, may hold values from 0 to 31
- block_cols: int32 [96, 64], P(('grp', 'blade'), 'dof'), parts along dimension 0, may hold values from 0 to 31
Outputs:
- spectral: float32 [2, 96, 512, 512], P(None, ('grp', 'blade'), 'dof'), parts along dimension 1
The draws below stay inside these ranges and needn't reach their ends.
There are 2 independent parts, one for each index of `grp`. The reference program is written for one: setup_inputs(seed, part) draws one part's arguments, and reference() takes and returns one part's arrays. A program takes and returns all parts, laid end to end along the dimension named above; each array names one. Nothing has to cross between parts.
Inputs may be any that keep to these rules, and one draw needn't show every extreme that they name: `block_rows`: row block index of each stiffness block; indices of one blade may repeat. `block_cols`: column block index of each stiffness block; indices of one blade may repeat.
All inputs are finite; a program needn't handle non-finite values.
Results may differ from the reference program's by a relative error of at most 0.0029.
Values may be sent and summed in bfloat16 or wider, within the bound.
No kernel may reach another device: no remote copies, remote signals or barrier semaphores. Data moves between devices by JAX's collectives and lax.ppermute only.
A program may use at most 128 MiB of HBM per device.

```python
import math
import jax
import jax.numpy as jnp
from jax import lax

M = 512
BS = 128
NDOF = 4096
BLADES = 48
NBLK = 64


def place_ends(array, rng, low, high):
    index_at = [jax.random.randint(jax.random.fold_in(rng, axis), (), 0, length) for axis, length in enumerate(array.shape)]
    longest = array.shape.index(max(array.shape))
    neighbour = index_at[:longest] + [(index_at[longest] + 1) % array.shape[longest]] + index_at[longest + 1:]
    return array.at[tuple(index_at)].set(low).at[tuple(neighbour)].set(high)


def level_of(stream_key, shape, pieces, low, largest):
    loudness, own = 1.0, jax.random.fold_in(stream_key, 6)
    for position, shards_of in pieces:
        draws = jnp.exp(jax.random.uniform(jax.random.fold_in(own, position), (shards_of,), jnp.float32, low / len(pieces), largest / len(pieces)))
        loudness = loudness * jnp.repeat(draws, shape[position] // shards_of).reshape([-1 if axis == position else 1 for axis in range(len(shape))])
    return loudness


def scatter_about(own_key, extent, spread, reach, shards=(), held_as=jnp.bfloat16):
    factor_of = level_of(own_key, extent, shards, -0.22, 0.18) if shards else 1.0
    values = jax.random.normal(own_key, extent, jnp.float32) * spread * factor_of
    return jnp.minimum(jnp.maximum(values, -reach), reach).astype(held_as)


def setup_inputs(seed: int = 0, part: int = 0) -> dict:
    key_list = jax.random.split(jax.random.key(seed), 5)
    own_keys = jax.random.split(jax.random.fold_in(key_list[4], part), 5)
    panel = scatter_about(own_keys[0], (NDOF, M), ((NBLK * BS * BLADES) ** -0.25), 0.25, ((0, 16),))
    stiffness = scatter_about(own_keys[1], (BLADES, NBLK, BS, BS), BS ** -0.5, 0.5, ((0, 8), (1, 2)))
    block_rows = place_ends(jax.random.randint(own_keys[2], (BLADES, NBLK), 0, NDOF // BS), jax.random.fold_in(own_keys[2], 1), 0, (NDOF // BS) - 1).astype(jnp.int32)
    block_cols = place_ends(jax.random.randint(own_keys[3], (BLADES, NBLK), 0, NDOF // BS), jax.random.fold_in(own_keys[3], 1), 0, (NDOF // BS) - 1).astype(jnp.int32)
    return dict(panel=panel, stiffness=stiffness, block_rows=block_rows, block_cols=block_cols)


def reference(panel, stiffness, block_rows, block_cols):
    blocks = panel.astype(jnp.float32).reshape(NDOF // BS, BS, M)

    def one_blade(items):
        mats, rows, cols = items
        chosen = blocks[cols]
        image = jnp.einsum("nij,njm->nim", mats.astype(jnp.float32), chosen, precision=lax.Precision.HIGHEST)
        image = image.astype(jnp.bfloat16).astype(jnp.float32)
        left = blocks[rows].reshape(-1, M)
        return jnp.dot(left.T, image.reshape(-1, M), precision=lax.Precision.HIGHEST)

    projected = lax.map(one_blade, (stiffness, block_rows, block_cols))
    index = jnp.arange(BLADES, dtype=jnp.int32)
    angle = ((index[:, None] * index[None, :]) % BLADES).astype(jnp.float32) * (2.0 * math.pi / BLADES)
    real_part = jnp.einsum("hb,brc->hrc", jnp.cos(angle), projected, precision=lax.Precision.HIGHEST)
    imag_part = -jnp.einsum("hb,brc->hrc", jnp.sin(angle), projected, precision=lax.Precision.HIGHEST)
    return jnp.stack([real_part, imag_part])
```

```python
import math

import jax
import jax.numpy as jnp
from jax import lax
from jax.experimental import pallas as pl
from jax.experimental.pallas import tpu as pltpu
from jax.sharding import PartitionSpec as P


def _project_kernel(rows_ref, cols_ref, pb_ref, pt_ref, s_ref, o_ref, lt_ref, img_ref):
    b = pl.program_id(0)
    nblk = s_ref.shape[1]
    bs = s_ref.shape[2]
    last = pb_ref.shape[0] - 1
    for n in range(nblk):
        c = jnp.minimum(jnp.maximum(cols_ref[b * nblk + n], 0), last)
        r = jnp.minimum(jnp.maximum(rows_ref[b * nblk + n], 0), last)
        im = jnp.dot(s_ref[0, n], pb_ref[c], preferred_element_type=jnp.float32)
        img_ref[n * bs:(n + 1) * bs, :] = im.astype(jnp.bfloat16)
        lt_ref[:, n * bs:(n + 1) * bs] = pt_ref[r]
    o_ref[0] = jnp.dot(lt_ref[...], img_ref[...], preferred_element_type=jnp.float32)


def _project(pb, pt, stiffness, rows, cols):
    nbl, nblk, bs, _ = stiffness.shape
    nrb, _, modes = pb.shape
    grid_spec = pltpu.PrefetchScalarGridSpec(
        num_scalar_prefetch=2,
        grid=(nbl,),
        in_specs=[
            pl.BlockSpec((nrb, bs, modes), lambda b, rr, cc: (0, 0, 0)),
            pl.BlockSpec((nrb, modes, bs), lambda b, rr, cc: (0, 0, 0)),
            pl.BlockSpec((1, nblk, bs, bs), lambda b, rr, cc: (b, 0, 0, 0)),
        ],
        out_specs=pl.BlockSpec((1, modes, modes), lambda b, rr, cc: (b, 0, 0)),
        scratch_shapes=[
            pltpu.VMEM((modes, nblk * bs), jnp.bfloat16),
            pltpu.VMEM((nblk * bs, modes), jnp.bfloat16),
        ],
    )
    return pl.pallas_call(
        _project_kernel,
        grid_spec=grid_spec,
        out_shape=jax.ShapeDtypeStruct((nbl, modes, modes), jnp.float32),
        compiler_params=pltpu.CompilerParams(
            dimension_semantics=("arbitrary",),
            vmem_limit_bytes=56 * 1024 * 1024,
        ),
    )(rows, cols, pb, pt, stiffness)


def _trig(h, b, count):
    angle = ((h * b) % count).astype(jnp.float32) * (2.0 * math.pi / count)
    return jnp.cos(angle), -jnp.sin(angle)


def body(panel, stiffness, block_rows, block_cols):
    nbl, nblk, bs, _ = stiffness.shape
    modes = panel.shape[-1]
    whole = lax.all_gather(panel, ("blade", "dof"), axis=0, tiled=True)
    pb = whole.reshape(-1, bs, modes)
    pt = jnp.swapaxes(pb, 1, 2)
    proj = _project(pb, pt, stiffness, block_rows.reshape(-1), block_cols.reshape(-1))

    half = lax.psum_scatter(proj, "dof", scatter_dimension=1, tiled=True)
    nbd = lax.axis_size("blade")
    me = lax.axis_index("blade")
    rows_half = half.shape[1]
    r = rows_half // nbd
    chunks = half.reshape(nbl, nbd, r, modes)

    got = []
    for s in range(nbd):
        piece = lax.dynamic_index_in_dim(chunks, (me + s) % nbd, axis=1, keepdims=False)
        if s:
            piece = lax.ppermute(piece, "blade", [(j, (j + s) % nbd) for j in range(nbd)])
        got.append(piece)
    stacked = jnp.stack(got).reshape(nbd * nbl, r * modes)

    count = nbl * nbd
    src = (me - jnp.arange(nbd, dtype=jnp.int32)) % nbd
    blade = (nbl * src[:, None] + jnp.arange(nbl, dtype=jnp.int32)[None, :]).reshape(-1)
    dst = (me + jnp.arange(nbd, dtype=jnp.int32)) % nbd
    harm = (nbl * dst[:, None] + jnp.arange(nbl, dtype=jnp.int32)[None, :]).reshape(-1)
    cosine, sine = _trig(harm[:, None], blade[None, :], count)
    weights = jnp.concatenate([cosine, sine], axis=0)
    spec = jnp.dot(weights, stacked, precision=lax.Precision.HIGHEST)
    spec = spec.reshape(2, nbd, nbl, r, modes)

    out = jnp.zeros((2, nbl, rows_half, modes), jnp.float32)
    for t in range(nbd):
        piece = spec[:, t]
        if t:
            piece = lax.ppermute(piece, "blade", [(j, (j + t) % nbd) for j in range(nbd)])
        at = ((me - t) % nbd) * r
        out = lax.dynamic_update_slice(out, piece, (0, 0, at, 0))
    return out


def solution(mesh):
    placed = (
        P(("grp", "blade", "dof"), None),
        P(("grp", "blade"), "dof", None, None),
        P(("grp", "blade"), "dof"),
        P(("grp", "blade"), "dof"),
    )
    return jax.shard_map(
        body,
        mesh=mesh,
        in_specs=placed,
        out_specs=P(None, ("grp", "blade"), "dof", None),
        check_vma=False,
    )
```

```python
import math

import jax
import jax.numpy as jnp
from jax import lax
from jax.experimental import pallas as pl
from jax.experimental.pallas import tpu as pltpu
from jax.sharding import PartitionSpec as P


def _project_kernel(rows_ref, cols_ref, pb_ref, pt_ref, s_ref, o_ref, lt_ref, img_ref):
    b = pl.program_id(0)
    nblk = s_ref.shape[1]
    bs = s_ref.shape[2]
    last = pb_ref.shape[0] - 1
    for n in range(nblk):
        c = jnp.minimum(jnp.maximum(cols_ref[b * nblk + n], 0), last)
        r = jnp.minimum(jnp.maximum(rows_ref[b * nblk + n], 0), last)
        im = jnp.dot(s_ref[0, n], pb_ref[c], preferred_element_type=jnp.float32)
        img_ref[n * bs:(n + 1) * bs, :] = im.astype(jnp.bfloat16)
        lt_ref[:, n * bs:(n + 1) * bs] = pt_ref[r]
    o_ref[0] = jnp.dot(lt_ref[...], img_ref[...], preferred_element_type=jnp.float32)


def _project(pb, pt, stiffness, rows, cols):
    nbl, nblk, bs, _ = stiffness.shape
    nrb, _, modes = pb.shape
    grid_spec = pltpu.PrefetchScalarGridSpec(
        num_scalar_prefetch=2,
        grid=(nbl,),
        in_specs=[
            pl.BlockSpec((nrb, bs, modes), lambda b, rr, cc: (0, 0, 0)),
            pl.BlockSpec((nrb, modes, bs), lambda b, rr, cc: (0, 0, 0)),
            pl.BlockSpec((1, nblk, bs, bs), lambda b, rr, cc: (b, 0, 0, 0)),
        ],
        out_specs=pl.BlockSpec((1, modes, modes), lambda b, rr, cc: (b, 0, 0)),
        scratch_shapes=[
            pltpu.VMEM((modes, nblk * bs), jnp.bfloat16),
            pltpu.VMEM((nblk * bs, modes), jnp.bfloat16),
        ],
    )
    return pl.pallas_call(
        _project_kernel,
        grid_spec=grid_spec,
        out_shape=jax.ShapeDtypeStruct((nbl, modes, modes), jnp.float32),
        compiler_params=pltpu.CompilerParams(
            dimension_semantics=("arbitrary",),
            vmem_limit_bytes=56 * 1024 * 1024,
        ),
    )(rows, cols, pb, pt, stiffness)


def _dft_kernel(wh_ref, wl_ref, x_ref, o_ref):
    x = x_ref[...]
    xh = x.astype(jnp.bfloat16)
    xl = (x - xh.astype(jnp.float32)).astype(jnp.bfloat16)
    wh = wh_ref[...]
    acc = jnp.dot(wh, xh, preferred_element_type=jnp.float32)
    acc += jnp.dot(wh, xl, preferred_element_type=jnp.float32)
    acc += jnp.dot(wl_ref[...], xh, preferred_element_type=jnp.float32)
    o_ref[...] = acc


def _dft(weights, x):
    rows, k = weights.shape
    n = x.shape[1]
    wh = weights.astype(jnp.bfloat16)
    wl = (weights - wh.astype(jnp.float32)).astype(jnp.bfloat16)
    tn = 2048 if n % 2048 == 0 else n
    return pl.pallas_call(
        _dft_kernel,
        grid=(n // tn,),
        in_specs=[
            pl.BlockSpec((rows, k), lambda i: (0, 0)),
            pl.BlockSpec((rows, k), lambda i: (0, 0)),
            pl.BlockSpec((k, tn), lambda i: (0, i)),
        ],
        out_specs=pl.BlockSpec((rows, tn), lambda i: (0, i)),
        out_shape=jax.ShapeDtypeStruct((rows, n), jnp.float32),
        compiler_params=pltpu.CompilerParams(dimension_semantics=("arbitrary",)),
    )(wh, wl, x)


def _trig(h, b, count):
    angle = ((h * b) % count).astype(jnp.float32) * (2.0 * math.pi / count)
    return jnp.cos(angle), -jnp.sin(angle)


def body(panel, stiffness, block_rows, block_cols):
    nbl, nblk, bs, _ = stiffness.shape
    modes = panel.shape[-1]
    nbd = lax.axis_size("blade")
    nd = lax.axis_size("dof")
    whole = lax.all_gather(panel, "blade", axis=0, tiled=True)
    whole = lax.all_gather(whole, "dof", axis=0, tiled=True)
    pb = whole.reshape(-1, bs, modes)
    pt = jnp.swapaxes(pb, 1, 2)
    bpd = panel.shape[0] // bs

    def remap(j):
        j = jnp.clip(j.reshape(-1), 0, pb.shape[0] - 1)
        k = j // bpd
        return ((k % nd) * nbd + k // nd) * bpd + j % bpd

    proj = _project(pb, pt, stiffness, remap(block_rows), remap(block_cols))

    half = lax.psum_scatter(proj, "dof", scatter_dimension=1, tiled=True)
    me = lax.axis_index("blade")
    rows_half = half.shape[1]
    r = rows_half // nbd
    chunks = half.reshape(nbl, nbd, r, modes)

    got = []
    for s in range(nbd):
        piece = lax.dynamic_index_in_dim(chunks, (me + s) % nbd, axis=1, keepdims=False)
        if s:
            piece = lax.ppermute(piece, "blade", [(j, (j + s) % nbd) for j in range(nbd)])
        got.append(piece)
    stacked = jnp.stack(got).reshape(nbd * nbl, r * modes)

    count = nbl * nbd
    src = (me - jnp.arange(nbd, dtype=jnp.int32)) % nbd
    blade = (nbl * src[:, None] + jnp.arange(nbl, dtype=jnp.int32)[None, :]).reshape(-1)
    dst = (me + jnp.arange(nbd, dtype=jnp.int32)) % nbd
    harm = (nbl * dst[:, None] + jnp.arange(nbl, dtype=jnp.int32)[None, :]).reshape(-1)
    cosine, sine = _trig(harm[:, None], blade[None, :], count)
    weights = jnp.stack([cosine.reshape(nbd, nbl, -1), sine.reshape(nbd, nbl, -1)], axis=1)
    spec = _dft(weights.reshape(2 * count, count), stacked)
    spec = spec.reshape(nbd, 2, nbl, r, modes)

    out = jnp.zeros((2, nbl, rows_half, modes), jnp.float32)
    for t in range(nbd):
        piece = spec[t]
        if t:
            piece = lax.ppermute(piece, "blade", [(j, (j + t) % nbd) for j in range(nbd)])
        at = ((me - t) % nbd) * r
        out = lax.dynamic_update_slice(out, piece, (0, 0, at, 0))
    return out


def solution(mesh):
    placed = (
        P(("grp", "blade", "dof"), None),
        P(("grp", "blade"), "dof", None, None),
        P(("grp", "blade"), "dof"),
        P(("grp", "blade"), "dof"),
    )
    return jax.shard_map(
        body,
        mesh=mesh,
        in_specs=placed,
        out_specs=P(None, ("grp", "blade"), "dof", None),
        check_vma=False,
    )
```

```python
import math

import jax
import jax.numpy as jnp
from jax import lax
from jax.experimental import pallas as pl
from jax.experimental.pallas import tpu as pltpu
from jax.sharding import PartitionSpec as P


def _project_kernel(rows_ref, cols_ref, pb_ref, pt_ref, s_ref, o_ref, lt_ref, img_ref):
    b = pl.program_id(0)
    nblk = s_ref.shape[1]
    bs = s_ref.shape[2]
    last = pb_ref.shape[0] - 1
    for n in range(nblk):
        c = jnp.minimum(jnp.maximum(cols_ref[b * nblk + n], 0), last)
        r = jnp.minimum(jnp.maximum(rows_ref[b * nblk + n], 0), last)
        im = jnp.dot(s_ref[0, n], pb_ref[c], preferred_element_type=jnp.float32)
        img_ref[n * bs:(n + 1) * bs, :] = im.astype(jnp.bfloat16)
        lt_ref[:, n * bs:(n + 1) * bs] = pt_ref[r]
    o_ref[0] = jnp.dot(lt_ref[...], img_ref[...], preferred_element_type=jnp.float32)


def _project(pb, pt, stiffness, rows, cols):
    nbl, nblk, bs, _ = stiffness.shape
    nrb, _, modes = pb.shape
    grid_spec = pltpu.PrefetchScalarGridSpec(
        num_scalar_prefetch=2,
        grid=(nbl,),
        in_specs=[
            pl.BlockSpec((nrb, bs, modes), lambda b, rr, cc: (0, 0, 0)),
            pl.BlockSpec((nrb, modes, bs), lambda b, rr, cc: (0, 0, 0)),
            pl.BlockSpec((1, nblk, bs, bs), lambda b, rr, cc: (b, 0, 0, 0)),
        ],
        out_specs=pl.BlockSpec((1, modes, modes), lambda b, rr, cc: (b, 0, 0)),
        scratch_shapes=[
            pltpu.VMEM((modes, nblk * bs), jnp.bfloat16),
            pltpu.VMEM((nblk * bs, modes), jnp.bfloat16),
        ],
    )
    return pl.pallas_call(
        _project_kernel,
        grid_spec=grid_spec,
        out_shape=jax.ShapeDtypeStruct((nbl, modes, modes), jnp.float32),
        compiler_params=pltpu.CompilerParams(
            dimension_semantics=("arbitrary",),
            vmem_limit_bytes=56 * 1024 * 1024,
        ),
    )(rows, cols, pb, pt, stiffness)


def _dft_kernel(w_ref, x_ref, o_ref):
    x = x_ref[...]
    xh = x.astype(jnp.bfloat16)
    xl = (x - xh.astype(jnp.float32)).astype(jnp.bfloat16)
    w = w_ref[...]
    wh = w.astype(jnp.bfloat16)
    wl = (w - wh.astype(jnp.float32)).astype(jnp.bfloat16)
    acc = jnp.dot(wh, xh, preferred_element_type=jnp.float32)
    acc += jnp.dot(wh, xl, preferred_element_type=jnp.float32)
    acc += jnp.dot(wl, xh, preferred_element_type=jnp.float32)
    o_ref[...] = acc


def _dft(weights, x):
    rows, k = weights.shape
    n = x.shape[1]
    tn = 2048 if n % 2048 == 0 else n
    return pl.pallas_call(
        _dft_kernel,
        grid=(n // tn,),
        in_specs=[
            pl.BlockSpec((rows, k), lambda i: (0, 0)),
            pl.BlockSpec((k, tn), lambda i: (0, i)),
        ],
        out_specs=pl.BlockSpec((rows, tn), lambda i: (0, i)),
        out_shape=jax.ShapeDtypeStruct((rows, n), jnp.float32),
        compiler_params=pltpu.CompilerParams(dimension_semantics=("arbitrary",)),
    )(weights, x)


def _trig(h, b, count):
    angle = ((h * b) % count).astype(jnp.float32) * (2.0 * math.pi / count)
    return jnp.cos(angle), -jnp.sin(angle)


def body(panel, stiffness, block_rows, block_cols):
    nbl, nblk, bs, _ = stiffness.shape
    modes = panel.shape[-1]
    nbd = lax.axis_size("blade")
    nd = lax.axis_size("dof")
    whole = lax.all_gather(panel, "blade", axis=0, tiled=True)
    whole = lax.all_gather(whole, "dof", axis=0, tiled=True)
    pb = whole.reshape(-1, bs, modes)
    pt = jnp.swapaxes(pb, 1, 2)
    bpd = panel.shape[0] // bs

    def remap(j):
        j = jnp.clip(j.reshape(-1), 0, pb.shape[0] - 1)
        k = j // bpd
        return ((k % nd) * nbd + k // nd) * bpd + j % bpd

    proj = _project(pb, pt, stiffness, remap(block_rows), remap(block_cols))

    half = lax.psum_scatter(proj, "dof", scatter_dimension=1, tiled=True)
    me = lax.axis_index("blade")
    rows_half = half.shape[1]
    groups = 2 if nbd % 2 == 0 and rows_half % (nbd // 2) == 0 else 1
    per = nbd // groups
    r = rows_half // per
    chunks = half.reshape(nbl, per, r, modes)

    got = []
    for s in range(nbd):
        piece = lax.dynamic_index_in_dim(chunks, ((me + s) % nbd) % per, axis=1, keepdims=False)
        if s:
            piece = lax.ppermute(piece, "blade", [(j, (j + s) % nbd) for j in range(nbd)])
        got.append(piece)
    stacked = jnp.stack(got).reshape(nbd * nbl, r * modes)

    count = nbl * nbd
    src = (me - jnp.arange(nbd, dtype=jnp.int32)) % nbd
    blade = (nbl * src[:, None] + jnp.arange(nbl, dtype=jnp.int32)[None, :]).reshape(-1)
    base = (me // per) * per
    dst = base + (me % per + jnp.arange(per, dtype=jnp.int32)) % per
    harm = (nbl * dst[:, None] + jnp.arange(nbl, dtype=jnp.int32)[None, :]).reshape(-1)
    cosine, sine = _trig(harm[:, None], blade[None, :], count)
    weights = jnp.stack([cosine.reshape(per, nbl, -1), sine.reshape(per, nbl, -1)], axis=1)
    spec = _dft(weights.reshape(2 * per * nbl, count), stacked)
    spec = spec.reshape(per, 2, nbl, r, modes)

    out = jnp.zeros((2, nbl, rows_half, modes), jnp.float32)
    for u in range(per):
        piece = spec[u]
        if u:
            pairs = [(j, (j // per) * per + (j % per + u) % per) for j in range(nbd)]
            piece = lax.ppermute(piece, "blade", pairs)
        at = ((me % per - u) % per) * r
        out = lax.dynamic_update_slice(out, piece, (0, 0, at, 0))
    return out


def solution(mesh):
    placed = (
        P(("grp", "blade", "dof"), None),
        P(("grp", "blade"), "dof", None, None),
        P(("grp", "blade"), "dof"),
        P(("grp", "blade"), "dof"),
    )
    return jax.shard_map(
        body,
        mesh=mesh,
        in_specs=placed,
        out_specs=P(None, ("grp", "blade"), "dof", None),
        check_vma=False,
    )
```

```python
import math

import jax
import jax.numpy as jnp
from jax import lax
from jax.experimental import pallas as pl
from jax.experimental.pallas import tpu as pltpu
from jax.sharding import PartitionSpec as P


def _project_kernel(rows_ref, cols_ref, pb_ref, pt_ref, s_ref, o_ref, lt_ref, img_ref):
    b = pl.program_id(0)
    nblk = s_ref.shape[1]
    bs = s_ref.shape[2]
    last = pb_ref.shape[0] - 1
    for n in range(nblk):
        c = jnp.minimum(jnp.maximum(cols_ref[b * nblk + n], 0), last)
        r = jnp.minimum(jnp.maximum(rows_ref[b * nblk + n], 0), last)
        im = jnp.dot(s_ref[0, n], pb_ref[c], preferred_element_type=jnp.float32)
        img_ref[n * bs:(n + 1) * bs, :] = im.astype(jnp.bfloat16)
        lt_ref[:, n * bs:(n + 1) * bs] = pt_ref[r]
    o_ref[0] = jnp.dot(lt_ref[...], img_ref[...], preferred_element_type=jnp.float32)


def _project(pb, pt, stiffness, rows, cols):
    nbl, nblk, bs, _ = stiffness.shape
    nrb, _, modes = pb.shape
    grid_spec = pltpu.PrefetchScalarGridSpec(
        num_scalar_prefetch=2,
        grid=(nbl,),
        in_specs=[
            pl.BlockSpec((nrb, bs, modes), lambda b, rr, cc: (0, 0, 0)),
            pl.BlockSpec((nrb, modes, bs), lambda b, rr, cc: (0, 0, 0)),
            pl.BlockSpec((1, nblk, bs, bs), lambda b, rr, cc: (b, 0, 0, 0)),
        ],
        out_specs=pl.BlockSpec((1, modes, modes), lambda b, rr, cc: (b, 0, 0)),
        scratch_shapes=[
            pltpu.VMEM((modes, nblk * bs), jnp.bfloat16),
            pltpu.VMEM((nblk * bs, modes), jnp.bfloat16),
        ],
    )
    return pl.pallas_call(
        _project_kernel,
        grid_spec=grid_spec,
        out_shape=jax.ShapeDtypeStruct((nbl, modes, modes), jnp.float32),
        compiler_params=pltpu.CompilerParams(
            dimension_semantics=("arbitrary",),
            vmem_limit_bytes=56 * 1024 * 1024,
        ),
    )(rows, cols, pb, pt, stiffness)


def _dft_kernel(w_ref, x_ref, o_ref):
    x = x_ref[...]
    xh = x.astype(jnp.bfloat16)
    xl = (x - xh.astype(jnp.float32)).astype(jnp.bfloat16)
    w = w_ref[...]
    wh = w.astype(jnp.bfloat16)
    wl = (w - wh.astype(jnp.float32)).astype(jnp.bfloat16)
    acc = jnp.dot(wh, xh, preferred_element_type=jnp.float32)
    acc += jnp.dot(wh, xl, preferred_element_type=jnp.float32)
    acc += jnp.dot(wl, xh, preferred_element_type=jnp.float32)
    o_ref[...] = acc


def _dft(weights, x):
    rows, k = weights.shape
    n = x.shape[1]
    tn = 2048 if n % 2048 == 0 else n
    return pl.pallas_call(
        _dft_kernel,
        grid=(n // tn,),
        in_specs=[
            pl.BlockSpec((rows, k), lambda i: (0, 0)),
            pl.BlockSpec((k, tn), lambda i: (0, i)),
        ],
        out_specs=pl.BlockSpec((rows, tn), lambda i: (0, i)),
        out_shape=jax.ShapeDtypeStruct((rows, n), jnp.float32),
        compiler_params=pltpu.CompilerParams(dimension_semantics=("arbitrary",)),
    )(weights, x)


def _trig(h, b, count):
    angle = ((h * b) % count).astype(jnp.float32) * (2.0 * math.pi / count)
    return jnp.cos(angle), -jnp.sin(angle)


def body(panel, stiffness, block_rows, block_cols):
    nbl, nblk, bs, _ = stiffness.shape
    modes = panel.shape[-1]
    nbd = lax.axis_size("blade")
    whole = lax.all_gather(panel, ("blade", "dof"), axis=0, tiled=True)
    pb = whole.reshape(-1, bs, modes)
    pt = jnp.swapaxes(pb, 1, 2)
    proj = _project(pb, pt, stiffness, block_rows.reshape(-1), block_cols.reshape(-1))

    half = lax.psum_scatter(proj, "dof", scatter_dimension=1, tiled=True)
    me = lax.axis_index("blade")
    rows_half = half.shape[1]
    r = rows_half // nbd
    chunks = half.reshape(nbl, nbd, r, modes)

    got = []
    for s in range(nbd):
        piece = lax.dynamic_index_in_dim(chunks, (me + s) % nbd, axis=1, keepdims=False)
        if s:
            piece = lax.ppermute(piece, "blade", [(j, (j + s) % nbd) for j in range(nbd)])
        got.append(piece)
    stacked = jnp.stack(got).reshape(nbd * nbl, r * modes)

    count = nbl * nbd
    src = (me - jnp.arange(nbd, dtype=jnp.int32)) % nbd
    blade = (nbl * src[:, None] + jnp.arange(nbl, dtype=jnp.int32)[None, :]).reshape(-1)
    dst = (me + jnp.arange(nbd, dtype=jnp.int32)) % nbd
    harm = (nbl * dst[:, None] + jnp.arange(nbl, dtype=jnp.int32)[None, :]).reshape(-1)
    cosine, sine = _trig(harm[:, None], blade[None, :], count)
    weights = jnp.stack([cosine.reshape(nbd, nbl, -1), sine.reshape(nbd, nbl, -1)], axis=1)
    spec = _dft(weights.reshape(2 * count, count), stacked)
    spec = spec.reshape(nbd, 2, nbl, r, modes)

    out = jnp.zeros((2, nbl, rows_half, modes), jnp.float32)
    for t in range(nbd):
        piece = spec[t]
        if t:
            piece = lax.ppermute(piece, "blade", [(j, (j + t) % nbd) for j in range(nbd)])
        at = ((me - t) % nbd) * r
        out = lax.dynamic_update_slice(out, piece, (0, 0, at, 0))
    return out


def solution(mesh):
    placed = (
        P(("grp", "blade", "dof"), None),
        P(("grp", "blade"), "dof", None, None),
        P(("grp", "blade"), "dof"),
        P(("grp", "blade"), "dof"),
    )
    return jax.shard_map(
        body,
        mesh=mesh,
        in_specs=placed,
        out_specs=P(None, ("grp", "blade"), "dof", None),
        check_vma=False,
    )
```

```python
import math

import jax
import jax.numpy as jnp
from jax import lax
from jax.experimental import pallas as pl
from jax.experimental.pallas import tpu as pltpu
from jax.sharding import PartitionSpec as P


def _project_kernel(rows_ref, cols_ref, pb_ref, pt_ref, s_ref, o_ref, lt_ref, img_ref):
    b = pl.program_id(0)
    nblk = s_ref.shape[1]
    bs = s_ref.shape[2]
    last = pb_ref.shape[0] - 1
    for n in range(nblk):
        c = jnp.minimum(jnp.maximum(cols_ref[b * nblk + n], 0), last)
        r = jnp.minimum(jnp.maximum(rows_ref[b * nblk + n], 0), last)
        im = jnp.dot(s_ref[0, n], pb_ref[c], preferred_element_type=jnp.float32)
        img_ref[n * bs:(n + 1) * bs, :] = im.astype(jnp.bfloat16)
        lt_ref[:, n * bs:(n + 1) * bs] = pt_ref[r]
    o_ref[0] = jnp.dot(lt_ref[...], img_ref[...], preferred_element_type=jnp.float32)


def _project(pb, pt, stiffness, rows, cols, start, nbl):
    _, nblk, bs, _ = stiffness.shape
    nrb, _, modes = pb.shape
    rows = rows[start * nblk:(start + nbl) * nblk]
    cols = cols[start * nblk:(start + nbl) * nblk]
    grid_spec = pltpu.PrefetchScalarGridSpec(
        num_scalar_prefetch=2,
        grid=(nbl,),
        in_specs=[
            pl.BlockSpec((nrb, bs, modes), lambda b, rr, cc: (0, 0, 0)),
            pl.BlockSpec((nrb, modes, bs), lambda b, rr, cc: (0, 0, 0)),
            pl.BlockSpec((1, nblk, bs, bs), lambda b, rr, cc: (b + start, 0, 0, 0)),
        ],
        out_specs=pl.BlockSpec((1, modes, modes), lambda b, rr, cc: (b, 0, 0)),
        scratch_shapes=[
            pltpu.VMEM((modes, nblk * bs), jnp.bfloat16),
            pltpu.VMEM((nblk * bs, modes), jnp.bfloat16),
        ],
    )
    return pl.pallas_call(
        _project_kernel,
        grid_spec=grid_spec,
        out_shape=jax.ShapeDtypeStruct((nbl, modes, modes), jnp.float32),
        compiler_params=pltpu.CompilerParams(
            dimension_semantics=("arbitrary",),
            vmem_limit_bytes=56 * 1024 * 1024,
        ),
    )(rows, cols, pb, pt, stiffness)


def _dft_kernel(w_ref, x_ref, o_ref):
    x = x_ref[...]
    xh = x.astype(jnp.bfloat16)
    xl = (x - xh.astype(jnp.float32)).astype(jnp.bfloat16)
    w = w_ref[...]
    wh = w.astype(jnp.bfloat16)
    wl = (w - wh.astype(jnp.float32)).astype(jnp.bfloat16)
    acc = jnp.dot(wh, xh, preferred_element_type=jnp.float32)
    acc += jnp.dot(wh, xl, preferred_element_type=jnp.float32)
    acc += jnp.dot(wl, xh, preferred_element_type=jnp.float32)
    o_ref[...] = acc


def _dft(weights, x):
    rows, k = weights.shape
    n = x.shape[1]
    tn = 2048 if n % 2048 == 0 else n
    return pl.pallas_call(
        _dft_kernel,
        grid=(n // tn,),
        in_specs=[
            pl.BlockSpec((rows, k), lambda i: (0, 0)),
            pl.BlockSpec((k, tn), lambda i: (0, i)),
        ],
        out_specs=pl.BlockSpec((rows, tn), lambda i: (0, i)),
        out_shape=jax.ShapeDtypeStruct((rows, n), jnp.float32),
        compiler_params=pltpu.CompilerParams(dimension_semantics=("arbitrary",)),
    )(weights, x)


def _trig(h, b, count):
    angle = ((h * b) % count).astype(jnp.float32) * (2.0 * math.pi / count)
    return jnp.cos(angle), -jnp.sin(angle)


def body(panel, stiffness, block_rows, block_cols):
    nbl, nblk, bs, _ = stiffness.shape
    modes = panel.shape[-1]
    nbd = lax.axis_size("blade")
    whole = lax.all_gather(panel, ("blade", "dof"), axis=0, tiled=True)
    pb = whole.reshape(-1, bs, modes)
    pt = jnp.swapaxes(pb, 1, 2)
    rows_all = block_rows.reshape(-1)
    cols_all = block_cols.reshape(-1)
    me = lax.axis_index("blade")
    rows_half = modes // lax.axis_size("dof")
    r = rows_half // nbd

    groups = 2 if nbl % 2 == 0 else 1
    size = nbl // groups
    parts = [[] for _ in range(nbd)]
    for g in range(groups):
        proj = _project(pb, pt, stiffness, rows_all, cols_all, g * size, size)
        half = lax.psum_scatter(proj, "dof", scatter_dimension=1, tiled=True)
        chunks = half.reshape(size, nbd, r, modes)
        for s in range(nbd):
            piece = lax.dynamic_index_in_dim(chunks, (me + s) % nbd, axis=1, keepdims=False)
            if s:
                piece = lax.ppermute(piece, "blade", [(j, (j + s) % nbd) for j in range(nbd)])
            parts[s].append(piece)
    got = [jnp.concatenate(p, axis=0) if len(p) > 1 else p[0] for p in parts]
    stacked = jnp.stack(got).reshape(nbd * nbl, r * modes)

    count = nbl * nbd
    src = (me - jnp.arange(nbd, dtype=jnp.int32)) % nbd
    blade = (nbl * src[:, None] + jnp.arange(nbl, dtype=jnp.int32)[None, :]).reshape(-1)
    dst = (me + jnp.arange(nbd, dtype=jnp.int32)) % nbd
    harm = (nbl * dst[:, None] + jnp.arange(nbl, dtype=jnp.int32)[None, :]).reshape(-1)
    cosine, sine = _trig(harm[:, None], blade[None, :], count)
    weights = jnp.stack([cosine.reshape(nbd, nbl, -1), sine.reshape(nbd, nbl, -1)], axis=1)
    spec = _dft(weights.reshape(2 * count, count), stacked)
    spec = spec.reshape(nbd, 2, nbl, r, modes)

    out = jnp.zeros((2, nbl, rows_half, modes), jnp.float32)
    for t in range(nbd):
        piece = spec[t]
        if t:
            piece = lax.ppermute(piece, "blade", [(j, (j + t) % nbd) for j in range(nbd)])
        at = ((me - t) % nbd) * r
        out = lax.dynamic_update_slice(out, piece, (0, 0, at, 0))
    return out


def solution(mesh):
    placed = (
        P(("grp", "blade", "dof"), None),
        P(("grp", "blade"), "dof", None, None),
        P(("grp", "blade"), "dof"),
        P(("grp", "blade"), "dof"),
    )
    return jax.shard_map(
        body,
        mesh=mesh,
        in_specs=placed,
        out_specs=P(None, ("grp", "blade"), "dof", None),
        check_vma=False,
    )
```

```python
import math

import jax
import jax.numpy as jnp
from jax import lax
from jax.experimental import pallas as pl
from jax.experimental.pallas import tpu as pltpu
from jax.sharding import PartitionSpec as P


def _project_kernel(rows_ref, cols_ref, pb_ref, pt_ref, s_ref, o_ref, lt_ref, img_ref):
    b = pl.program_id(0)
    nblk = s_ref.shape[1]
    bs = s_ref.shape[2]
    last = pb_ref.shape[0] - 1
    for n in range(nblk):
        c = jnp.minimum(jnp.maximum(cols_ref[b * nblk + n], 0), last)
        r = jnp.minimum(jnp.maximum(rows_ref[b * nblk + n], 0), last)
        im = jnp.dot(s_ref[0, n], pb_ref[c], preferred_element_type=jnp.float32)
        img_ref[n * bs:(n + 1) * bs, :] = im.astype(jnp.bfloat16)
        lt_ref[:, n * bs:(n + 1) * bs] = pt_ref[r]
    o_ref[0] = jnp.dot(lt_ref[...], img_ref[...], preferred_element_type=jnp.float32)


def _project(pb, pt, stiffness, rows, cols):
    nbl, nblk, bs, _ = stiffness.shape
    nrb, _, modes = pb.shape
    grid_spec = pltpu.PrefetchScalarGridSpec(
        num_scalar_prefetch=2,
        grid=(nbl,),
        in_specs=[
            pl.BlockSpec((nrb, bs, modes), lambda b, rr, cc: (0, 0, 0)),
            pl.BlockSpec((nrb, modes, bs), lambda b, rr, cc: (0, 0, 0)),
            pl.BlockSpec((1, nblk, bs, bs), lambda b, rr, cc: (b, 0, 0, 0)),
        ],
        out_specs=pl.BlockSpec((1, modes, modes), lambda b, rr, cc: (b, 0, 0)),
        scratch_shapes=[
            pltpu.VMEM((modes, nblk * bs), jnp.bfloat16),
            pltpu.VMEM((nblk * bs, modes), jnp.bfloat16),
        ],
    )
    return pl.pallas_call(
        _project_kernel,
        grid_spec=grid_spec,
        out_shape=jax.ShapeDtypeStruct((nbl, modes, modes), jnp.float32),
        compiler_params=pltpu.CompilerParams(
            dimension_semantics=("arbitrary",),
            vmem_limit_bytes=56 * 1024 * 1024,
        ),
    )(rows, cols, pb, pt, stiffness)


def _dft_kernel(w_ref, x_ref, o_ref):
    x = x_ref[...]
    xh = x.astype(jnp.bfloat16)
    xl = (x - xh.astype(jnp.float32)).astype(jnp.bfloat16)
    w = w_ref[...]
    wh = w.astype(jnp.bfloat16)
    wl = (w - wh.astype(jnp.float32)).astype(jnp.bfloat16)
    acc = jnp.dot(wh, xh, preferred_element_type=jnp.float32)
    acc += jnp.dot(wh, xl, preferred_element_type=jnp.float32)
    acc += jnp.dot(wl, xh, preferred_element_type=jnp.float32)
    o_ref[...] = acc


def _dft(weights, x):
    rows, k = weights.shape
    n = x.shape[1]
    tn = 2048 if n % 2048 == 0 else n
    return pl.pallas_call(
        _dft_kernel,
        grid=(n // tn,),
        in_specs=[
            pl.BlockSpec((rows, k), lambda i: (0, 0)),
            pl.BlockSpec((k, tn), lambda i: (0, i)),
        ],
        out_specs=pl.BlockSpec((rows, tn), lambda i: (0, i)),
        out_shape=jax.ShapeDtypeStruct((rows, n), jnp.float32),
        compiler_params=pltpu.CompilerParams(dimension_semantics=("arbitrary",)),
    )(weights, x)


def _trig(h, b, count):
    angle = ((h * b) % count).astype(jnp.float32) * (2.0 * math.pi / count)
    return jnp.cos(angle), -jnp.sin(angle)


def _ring_gather(x, nbd):
    me = lax.axis_index("blade")
    if nbd % 2 == 0:
        cycle = [2 * z for z in range(nbd // 2)] + [2 * z + 1 for z in reversed(range(nbd // 2))]
    else:
        cycle = list(range(nbd))
    place = [0] * nbd
    for q, j in enumerate(cycle):
        place[j] = q
    at = jnp.array(place, jnp.int32)[me]
    order = jnp.array(cycle, jnp.int32)
    fwd = [(cycle[q], cycle[(q + 1) % nbd]) for q in range(nbd)]
    bwd = [(cycle[q], cycle[(q - 1) % nbd]) for q in range(nbd)]
    buf = jnp.zeros((nbd,) + x.shape, x.dtype)
    buf = lax.dynamic_update_slice(buf, x[None], (me, 0, 0))
    ahead = nbd // 2
    behind = nbd - 1 - ahead
    a = x
    b = x
    for k in range(1, ahead + 1):
        a = lax.ppermute(a, "blade", fwd)
        buf = lax.dynamic_update_slice(buf, a[None], (order[(at - k) % nbd], 0, 0))
        if k <= behind:
            b = lax.ppermute(b, "blade", bwd)
            buf = lax.dynamic_update_slice(buf, b[None], (order[(at + k) % nbd], 0, 0))
    return buf


def body(panel, stiffness, block_rows, block_cols):
    nbl, nblk, bs, _ = stiffness.shape
    modes = panel.shape[-1]
    nbd = lax.axis_size("blade")
    nd = lax.axis_size("dof")
    whole = _ring_gather(panel, nbd)
    whole = lax.all_gather(whole, "dof", axis=0, tiled=True)
    pb = whole.reshape(-1, bs, modes)
    pt = jnp.swapaxes(pb, 1, 2)
    bpd = panel.shape[0] // bs

    def remap(j):
        j = jnp.clip(j.reshape(-1), 0, pb.shape[0] - 1)
        k = j // bpd
        return ((k % nd) * nbd + k // nd) * bpd + j % bpd

    proj = _project(pb, pt, stiffness, remap(block_rows), remap(block_cols))

    half = lax.psum_scatter(proj, "dof", scatter_dimension=1, tiled=True)
    me = lax.axis_index("blade")
    rows_half = half.shape[1]
    r = rows_half // nbd
    chunks = half.reshape(nbl, nbd, r, modes)

    got = []
    for s in range(nbd):
        piece = lax.dynamic_index_in_dim(chunks, (me + s) % nbd, axis=1, keepdims=False)
        if s:
            piece = lax.ppermute(piece, "blade", [(j, (j + s) % nbd) for j in range(nbd)])
        got.append(piece)
    stacked = jnp.stack(got).reshape(nbd * nbl, r * modes)

    count = nbl * nbd
    src = (me - jnp.arange(nbd, dtype=jnp.int32)) % nbd
    blade = (nbl * src[:, None] + jnp.arange(nbl, dtype=jnp.int32)[None, :]).reshape(-1)
    dst = (me + jnp.arange(nbd, dtype=jnp.int32)) % nbd
    harm = (nbl * dst[:, None] + jnp.arange(nbl, dtype=jnp.int32)[None, :]).reshape(-1)
    cosine, sine = _trig(harm[:, None], blade[None, :], count)
    weights = jnp.stack([cosine.reshape(nbd, nbl, -1), sine.reshape(nbd, nbl, -1)], axis=1)
    spec = _dft(weights.reshape(2 * count, count), stacked)
    spec = spec.reshape(nbd, 2, nbl, r, modes)

    out = jnp.zeros((2, nbl, rows_half, modes), jnp.float32)
    for t in range(nbd):
        piece = spec[t]
        if t:
            piece = lax.ppermute(piece, "blade", [(j, (j + t) % nbd) for j in range(nbd)])
        at = ((me - t) % nbd) * r
        out = lax.dynamic_update_slice(out, piece, (0, 0, at, 0))
    return out


def solution(mesh):
    placed = (
        P(("grp", "blade", "dof"), None),
        P(("grp", "blade"), "dof", None, None),
        P(("grp", "blade"), "dof"),
        P(("grp", "blade"), "dof"),
    )
    return jax.shard_map(
        body,
        mesh=mesh,
        in_specs=placed,
        out_specs=P(None, ("grp", "blade"), "dof", None),
        check_vma=False,
    )
```

```python
import math

import jax
import jax.numpy as jnp
from jax import lax
from jax.experimental import pallas as pl
from jax.experimental.pallas import tpu as pltpu
from jax.sharding import PartitionSpec as P


def _project_kernel(rows_ref, cols_ref, pb_ref, pt_ref, s_ref, o_ref, lt_ref, img_ref):
    b = pl.program_id(0)
    nblk = s_ref.shape[1]
    bs = s_ref.shape[2]
    last = pb_ref.shape[0] - 1
    for n in range(nblk):
        c = jnp.minimum(jnp.maximum(cols_ref[b * nblk + n], 0), last)
        r = jnp.minimum(jnp.maximum(rows_ref[b * nblk + n], 0), last)
        im = jnp.dot(s_ref[0, n], pb_ref[c], preferred_element_type=jnp.float32)
        img_ref[n * bs:(n + 1) * bs, :] = im.astype(jnp.bfloat16)
        lt_ref[:, n * bs:(n + 1) * bs] = pt_ref[r]
    o_ref[0] = jnp.dot(lt_ref[...], img_ref[...], preferred_element_type=jnp.float32)


def _project(pb, pt, stiffness, rows, cols):
    nbl, nblk, bs, _ = stiffness.shape
    nrb, _, modes = pb.shape
    grid_spec = pltpu.PrefetchScalarGridSpec(
        num_scalar_prefetch=2,
        grid=(nbl,),
        in_specs=[
            pl.BlockSpec((nrb, bs, modes), lambda b, rr, cc: (0, 0, 0)),
            pl.BlockSpec((nrb, modes, bs), lambda b, rr, cc: (0, 0, 0)),
            pl.BlockSpec((1, nblk, bs, bs), lambda b, rr, cc: (b, 0, 0, 0)),
        ],
        out_specs=pl.BlockSpec((1, modes, modes), lambda b, rr, cc: (b, 0, 0)),
        scratch_shapes=[
            pltpu.VMEM((modes, nblk * bs), jnp.bfloat16),
            pltpu.VMEM((nblk * bs, modes), jnp.bfloat16),
        ],
    )
    return pl.pallas_call(
        _project_kernel,
        grid_spec=grid_spec,
        out_shape=jax.ShapeDtypeStruct((nbl, modes, modes), jnp.float32),
        compiler_params=pltpu.CompilerParams(
            dimension_semantics=("arbitrary",),
            vmem_limit_bytes=56 * 1024 * 1024,
        ),
    )(rows, cols, pb, pt, stiffness)


def _dft_kernel(w_ref, x_ref, o_ref):
    r = x_ref.shape[1]
    w = w_ref[...]
    wh = w.astype(jnp.bfloat16)
    wl = (w - wh.astype(jnp.float32)).astype(jnp.bfloat16)

    def step(i, carry):
        x = x_ref[:, i, :]
        xh = x.astype(jnp.bfloat16)
        xl = (x - xh.astype(jnp.float32)).astype(jnp.bfloat16)
        acc = jnp.dot(wh, xh, preferred_element_type=jnp.float32)
        acc += jnp.dot(wh, xl, preferred_element_type=jnp.float32)
        acc += jnp.dot(wl, xh, preferred_element_type=jnp.float32)
        o_ref[:, i, :] = acc
        return carry

    lax.fori_loop(0, r, step, 0)


def _dft(weights, x):
    rows, k = weights.shape
    _, r, n = x.shape
    out = pl.pallas_call(
        _dft_kernel,
        out_shape=jax.ShapeDtypeStruct((rows, r, n), jnp.float32),
        compiler_params=pltpu.CompilerParams(vmem_limit_bytes=56 * 1024 * 1024),
    )(weights, x)
    return out


def _trig(h, b, count):
    angle = ((h * b) % count).astype(jnp.float32) * (2.0 * math.pi / count)
    return jnp.cos(angle), -jnp.sin(angle)


def body(panel, stiffness, block_rows, block_cols):
    nbl, nblk, bs, _ = stiffness.shape
    modes = panel.shape[-1]
    nbd = lax.axis_size("blade")
    whole = lax.all_gather(panel, ("blade", "dof"), axis=0, tiled=True)
    pb = whole.reshape(-1, bs, modes)
    pt = jnp.swapaxes(pb, 1, 2)
    proj = _project(pb, pt, stiffness, block_rows.reshape(-1), block_cols.reshape(-1))

    half = lax.psum_scatter(proj, "dof", scatter_dimension=1, tiled=True)
    me = lax.axis_index("blade")
    rows_half = half.shape[1]
    r = rows_half // nbd
    chunks = half.reshape(nbl, nbd, r, modes)

    got = []
    for s in range(nbd):
        piece = lax.dynamic_index_in_dim(chunks, (me + s) % nbd, axis=1, keepdims=False)
        if s:
            piece = lax.ppermute(piece, "blade", [(j, (j + s) % nbd) for j in range(nbd)])
        got.append(piece)
    stacked = jnp.stack(got).reshape(nbd * nbl, r, modes)

    count = nbl * nbd
    src = (me - jnp.arange(nbd, dtype=jnp.int32)) % nbd
    blade = (nbl * src[:, None] + jnp.arange(nbl, dtype=jnp.int32)[None, :]).reshape(-1)
    dst = (me + jnp.arange(nbd, dtype=jnp.int32)) % nbd
    harm = (nbl * dst[:, None] + jnp.arange(nbl, dtype=jnp.int32)[None, :]).reshape(-1)
    cosine, sine = _trig(harm[:, None], blade[None, :], count)
    weights = jnp.stack([cosine.reshape(nbd, nbl, -1), sine.reshape(nbd, nbl, -1)], axis=1)
    spec = _dft(weights.reshape(2 * count, count), stacked)
    spec = spec.reshape(nbd, 2, nbl, r, modes)

    out = jnp.zeros((2, nbl, rows_half, modes), jnp.float32)
    for t in range(nbd):
        piece = spec[t]
        if t:
            piece = lax.ppermute(piece, "blade", [(j, (j + t) % nbd) for j in range(nbd)])
        at = ((me - t) % nbd) * r
        out = lax.dynamic_update_slice(out, piece, (0, 0, at, 0))
    return out


def solution(mesh):
    placed = (
        P(("grp", "blade", "dof"), None),
        P(("grp", "blade"), "dof", None, None),
        P(("grp", "blade"), "dof"),
        P(("grp", "blade"), "dof"),
    )
    return jax.shard_map(
        body,
        mesh=mesh,
        in_specs=placed,
        out_specs=P(None, ("grp", "blade"), "dof", None),
        check_vma=False,
    )
```

```python
import math

import jax
import jax.numpy as jnp
from jax import lax
from jax.experimental import pallas as pl
from jax.experimental.pallas import tpu as pltpu
from jax.sharding import PartitionSpec as P


def _project_kernel(rows_ref, cols_ref, pb_ref, pt_ref, s_ref, o_ref, lt_ref, img_ref):
    b = pl.program_id(0)
    nblk = s_ref.shape[1]
    bs = s_ref.shape[2]
    last = pb_ref.shape[0] - 1
    for n in range(nblk):
        c = jnp.minimum(jnp.maximum(cols_ref[b * nblk + n], 0), last)
        r = jnp.minimum(jnp.maximum(rows_ref[b * nblk + n], 0), last)
        im = jnp.dot(s_ref[0, n], pb_ref[c], preferred_element_type=jnp.float32)
        img_ref[n * bs:(n + 1) * bs, :] = im.astype(jnp.bfloat16)
        lt_ref[:, n * bs:(n + 1) * bs] = pt_ref[r]
    o_ref[0] = jnp.dot(lt_ref[...], img_ref[...], preferred_element_type=jnp.float32)


def _project(pb, pt, stiffness, rows, cols):
    nbl, nblk, bs, _ = stiffness.shape
    nrb, _, modes = pb.shape
    grid_spec = pltpu.PrefetchScalarGridSpec(
        num_scalar_prefetch=2,
        grid=(nbl,),
        in_specs=[
            pl.BlockSpec((nrb, bs, modes), lambda b, rr, cc: (0, 0, 0)),
            pl.BlockSpec((nrb, modes, bs), lambda b, rr, cc: (0, 0, 0)),
            pl.BlockSpec((1, nblk, bs, bs), lambda b, rr, cc: (b, 0, 0, 0)),
        ],
        out_specs=pl.BlockSpec((1, modes, modes), lambda b, rr, cc: (b, 0, 0)),
        scratch_shapes=[
            pltpu.VMEM((modes, nblk * bs), jnp.bfloat16),
            pltpu.VMEM((nblk * bs, modes), jnp.bfloat16),
        ],
    )
    return pl.pallas_call(
        _project_kernel,
        grid_spec=grid_spec,
        out_shape=jax.ShapeDtypeStruct((nbl, modes, modes), jnp.float32),
        compiler_params=pltpu.CompilerParams(
            dimension_semantics=("arbitrary",),
            vmem_limit_bytes=56 * 1024 * 1024,
        ),
    )(rows, cols, pb, pt, stiffness)


def _dft_kernel(w_ref, x_ref, o_ref):
    x = x_ref[...]
    xh = x.astype(jnp.bfloat16)
    xl = (x - xh.astype(jnp.float32)).astype(jnp.bfloat16)
    w = w_ref[...]
    wh = w.astype(jnp.bfloat16)
    wl = (w - wh.astype(jnp.float32)).astype(jnp.bfloat16)
    acc = jnp.dot(wh, xh, preferred_element_type=jnp.float32)
    acc += jnp.dot(wh, xl, preferred_element_type=jnp.float32)
    acc += jnp.dot(wl, xh, preferred_element_type=jnp.float32)
    o_ref[...] = acc


def _dft(weights, x):
    rows, k = weights.shape
    n = x.shape[1]
    tn = 2048 if n % 2048 == 0 else n
    return pl.pallas_call(
        _dft_kernel,
        grid=(n // tn,),
        in_specs=[
            pl.BlockSpec((rows, k), lambda i: (0, 0)),
            pl.BlockSpec((k, tn), lambda i: (0, i)),
        ],
        out_specs=pl.BlockSpec((rows, tn), lambda i: (0, i)),
        out_shape=jax.ShapeDtypeStruct((rows, n), jnp.float32),
        compiler_params=pltpu.CompilerParams(dimension_semantics=("arbitrary",)),
    )(weights, x)


def _trig(h, b, count):
    angle = ((h * b) % count).astype(jnp.float32) * (2.0 * math.pi / count)
    return jnp.cos(angle), -jnp.sin(angle)


def body(panel, stiffness, block_rows, block_cols):
    nbl, nblk, bs, _ = stiffness.shape
    modes = panel.shape[-1]
    nbd = lax.axis_size("blade")
    whole = lax.all_gather(panel, ("blade", "dof"), axis=0, tiled=True)
    pb = whole.reshape(-1, bs, modes)
    pt = jnp.swapaxes(pb, 1, 2)
    proj = _project(pb, pt, stiffness, block_rows.reshape(-1), block_cols.reshape(-1))

    half = lax.psum_scatter(proj, "dof", scatter_dimension=1, tiled=True)
    me = lax.axis_index("blade")
    rows_half = half.shape[1]
    r = rows_half // nbd
    chunks = half.reshape(nbl, nbd, r, modes)

    got = []
    for s in range(nbd):
        piece = lax.dynamic_index_in_dim(chunks, (me + s) % nbd, axis=1, keepdims=False)
        if s:
            piece = lax.ppermute(piece, "blade", [(j, (j + s) % nbd) for j in range(nbd)])
        got.append(piece)
    stacked = jnp.stack(got).reshape(nbd * nbl, r * modes)

    count = nbl * nbd
    src = (me - jnp.arange(nbd, dtype=jnp.int32)) % nbd
    blade = (nbl * src[:, None] + jnp.arange(nbl, dtype=jnp.int32)[None, :]).reshape(-1)
    dst = (me + jnp.arange(nbd, dtype=jnp.int32)) % nbd
    harm = (nbl * dst[:, None] + jnp.arange(nbl, dtype=jnp.int32)[None, :]).reshape(-1)
    cosine, sine = _trig(harm[:, None], blade[None, :], count)
    weights = jnp.stack([cosine.reshape(nbd, nbl, -1), sine.reshape(nbd, nbl, -1)], axis=1)
    spec = _dft(weights.reshape(2 * count, count), stacked)
    spec = spec.reshape(nbd, 2, nbl, r, modes)

    out = jnp.zeros((2, nbl, rows_half, modes), jnp.float32)
    for t in range(nbd):
        piece = spec[t]
        if t:
            piece = piece.astype(jnp.bfloat16)
            piece = lax.ppermute(piece, "blade", [(j, (j + t) % nbd) for j in range(nbd)])
            piece = piece.astype(jnp.float32)
        at = ((me - t) % nbd) * r
        out = lax.dynamic_update_slice(out, piece, (0, 0, at, 0))
    return out


def solution(mesh):
    placed = (
        P(("grp", "blade", "dof"), None),
        P(("grp", "blade"), "dof", None, None),
        P(("grp", "blade"), "dof"),
        P(("grp", "blade"), "dof"),
    )
    return jax.shard_map(
        body,
        mesh=mesh,
        in_specs=placed,
        out_specs=P(None, ("grp", "blade"), "dof", None),
        check_vma=False,
    )
```

```python
import math

import jax
import jax.numpy as jnp
from jax import lax
from jax.experimental import pallas as pl
from jax.experimental.pallas import tpu as pltpu
from jax.sharding import PartitionSpec as P


def _project_kernel(rows_ref, cols_ref, pb_ref, pt_ref, s_ref, o_ref, lt_ref, img_ref):
    b = pl.program_id(0)
    nblk = s_ref.shape[1]
    bs = s_ref.shape[2]
    last = pb_ref.shape[0] - 1
    for n in range(nblk):
        c = jnp.minimum(jnp.maximum(cols_ref[b * nblk + n], 0), last)
        r = jnp.minimum(jnp.maximum(rows_ref[b * nblk + n], 0), last)
        im = jnp.dot(s_ref[0, n], pb_ref[c], preferred_element_type=jnp.float32)
        img_ref[n * bs:(n + 1) * bs, :] = im.astype(jnp.bfloat16)
        lt_ref[:, n * bs:(n + 1) * bs] = pt_ref[r]
    o_ref[0] = jnp.dot(lt_ref[...], img_ref[...], preferred_element_type=jnp.float32)


def _project(pb, pt, stiffness, rows, cols):
    nbl, nblk, bs, _ = stiffness.shape
    nrb, _, modes = pb.shape
    grid_spec = pltpu.PrefetchScalarGridSpec(
        num_scalar_prefetch=2,
        grid=(nbl,),
        in_specs=[
            pl.BlockSpec((nrb, bs, modes), lambda b, rr, cc: (0, 0, 0)),
            pl.BlockSpec((nrb, modes, bs), lambda b, rr, cc: (0, 0, 0)),
            pl.BlockSpec((1, nblk, bs, bs), lambda b, rr, cc: (b, 0, 0, 0)),
        ],
        out_specs=pl.BlockSpec((1, modes, modes), lambda b, rr, cc: (b, 0, 0)),
        scratch_shapes=[
            pltpu.VMEM((modes, nblk * bs), jnp.bfloat16),
            pltpu.VMEM((nblk * bs, modes), jnp.bfloat16),
        ],
    )
    return pl.pallas_call(
        _project_kernel,
        grid_spec=grid_spec,
        out_shape=jax.ShapeDtypeStruct((nbl, modes, modes), jnp.float32),
        compiler_params=pltpu.CompilerParams(
            dimension_semantics=("arbitrary",),
            vmem_limit_bytes=56 * 1024 * 1024,
        ),
    )(rows, cols, pb, pt, stiffness)


def _dft_kernel(w_ref, x_ref, o_ref):
    x = x_ref[...]
    xh = x.astype(jnp.bfloat16)
    xl = (x - xh.astype(jnp.float32)).astype(jnp.bfloat16)
    w = w_ref[...]
    wh = w.astype(jnp.bfloat16)
    wl = (w - wh.astype(jnp.float32)).astype(jnp.bfloat16)
    acc = jnp.dot(wh, xh, preferred_element_type=jnp.float32)
    acc += jnp.dot(wh, xl, preferred_element_type=jnp.float32)
    acc += jnp.dot(wl, xh, preferred_element_type=jnp.float32)
    o_ref[...] = acc


def _dft(weights, x):
    rows, k = weights.shape
    n = x.shape[1]
    tn = 2048 if n % 2048 == 0 else n
    return pl.pallas_call(
        _dft_kernel,
        grid=(n // tn,),
        in_specs=[
            pl.BlockSpec((rows, k), lambda i: (0, 0)),
            pl.BlockSpec((k, tn), lambda i: (0, i)),
        ],
        out_specs=pl.BlockSpec((rows, tn), lambda i: (0, i)),
        out_shape=jax.ShapeDtypeStruct((rows, n), jnp.float32),
        compiler_params=pltpu.CompilerParams(dimension_semantics=("arbitrary",)),
    )(weights, x)


def _trig(h, b, count):
    angle = ((h * b) % count).astype(jnp.float32) * (2.0 * math.pi / count)
    return jnp.cos(angle), -jnp.sin(angle)


def body(panel, stiffness, block_rows, block_cols):
    nbl, nblk, bs, _ = stiffness.shape
    modes = panel.shape[-1]
    nbd = lax.axis_size("blade")
    nd = lax.axis_size("dof")
    at = (lax.axis_index("blade") * nd + lax.axis_index("dof")) * panel.shape[0]
    whole = jnp.zeros((nbd * nd * panel.shape[0], modes), panel.dtype)
    whole = lax.psum(lax.dynamic_update_slice(whole, panel, (at, 0)), ("blade", "dof"))
    pb = whole.reshape(-1, bs, modes)
    pt = jnp.swapaxes(pb, 1, 2)
    proj = _project(pb, pt, stiffness, block_rows.reshape(-1), block_cols.reshape(-1))

    half = lax.psum_scatter(proj, "dof", scatter_dimension=1, tiled=True)
    me = lax.axis_index("blade")
    rows_half = half.shape[1]
    r = rows_half // nbd
    chunks = half.reshape(nbl, nbd, r, modes)

    got = []
    for s in range(nbd):
        piece = lax.dynamic_index_in_dim(chunks, (me + s) % nbd, axis=1, keepdims=False)
        if s:
            piece = lax.ppermute(piece, "blade", [(j, (j + s) % nbd) for j in range(nbd)])
        got.append(piece)
    stacked = jnp.stack(got).reshape(nbd * nbl, r * modes)

    count = nbl * nbd
    src = (me - jnp.arange(nbd, dtype=jnp.int32)) % nbd
    blade = (nbl * src[:, None] + jnp.arange(nbl, dtype=jnp.int32)[None, :]).reshape(-1)
    dst = (me + jnp.arange(nbd, dtype=jnp.int32)) % nbd
    harm = (nbl * dst[:, None] + jnp.arange(nbl, dtype=jnp.int32)[None, :]).reshape(-1)
    cosine, sine = _trig(harm[:, None], blade[None, :], count)
    weights = jnp.stack([cosine.reshape(nbd, nbl, -1), sine.reshape(nbd, nbl, -1)], axis=1)
    spec = _dft(weights.reshape(2 * count, count), stacked)
    spec = spec.reshape(nbd, 2, nbl, r, modes)

    out = jnp.zeros((2, nbl, rows_half, modes), jnp.float32)
    for t in range(nbd):
        piece = spec[t]
        if t:
            piece = piece.astype(jnp.bfloat16)
            piece = lax.ppermute(piece, "blade", [(j, (j + t) % nbd) for j in range(nbd)])
            piece = piece.astype(jnp.float32)
        at = ((me - t) % nbd) * r
        out = lax.dynamic_update_slice(out, piece, (0, 0, at, 0))
    return out


def solution(mesh):
    placed = (
        P(("grp", "blade", "dof"), None),
        P(("grp", "blade"), "dof", None, None),
        P(("grp", "blade"), "dof"),
        P(("grp", "blade"), "dof"),
    )
    return jax.shard_map(
        body,
        mesh=mesh,
        in_specs=placed,
        out_specs=P(None, ("grp", "blade"), "dof", None),
        check_vma=False,
    )
```

```python
import math

import jax
import jax.numpy as jnp
from jax import lax
from jax.experimental import pallas as pl
from jax.experimental.pallas import tpu as pltpu
from jax.sharding import PartitionSpec as P


_NT = (((1,), (1,)), ((), ()))


def _project_kernel(rows_ref, cols_ref, pt_ref, s_ref, o_ref, lt_ref, it_ref):
    b = pl.program_id(0)
    nblk = s_ref.shape[1]
    bs = s_ref.shape[2]
    last = pt_ref.shape[0] - 1
    for n in range(nblk):
        c = jnp.minimum(jnp.maximum(cols_ref[b * nblk + n], 0), last)
        r = jnp.minimum(jnp.maximum(rows_ref[b * nblk + n], 0), last)
        im = lax.dot_general(pt_ref[c], s_ref[0, n], _NT, preferred_element_type=jnp.float32)
        it_ref[:, n * bs:(n + 1) * bs] = im.astype(jnp.bfloat16)
        lt_ref[:, n * bs:(n + 1) * bs] = pt_ref[r]
    o_ref[0] = lax.dot_general(lt_ref[...], it_ref[...], _NT, preferred_element_type=jnp.float32)


def _project(pt, stiffness, rows, cols):
    nbl, nblk, bs, _ = stiffness.shape
    nrb, modes, _ = pt.shape
    grid_spec = pltpu.PrefetchScalarGridSpec(
        num_scalar_prefetch=2,
        grid=(nbl,),
        in_specs=[
            pl.BlockSpec((nrb, modes, bs), lambda b, rr, cc: (0, 0, 0)),
            pl.BlockSpec((1, nblk, bs, bs), lambda b, rr, cc: (b, 0, 0, 0)),
        ],
        out_specs=pl.BlockSpec((1, modes, modes), lambda b, rr, cc: (b, 0, 0)),
        scratch_shapes=[
            pltpu.VMEM((modes, nblk * bs), jnp.bfloat16),
            pltpu.VMEM((modes, nblk * bs), jnp.bfloat16),
        ],
    )
    return pl.pallas_call(
        _project_kernel,
        grid_spec=grid_spec,
        out_shape=jax.ShapeDtypeStruct((nbl, modes, modes), jnp.float32),
        compiler_params=pltpu.CompilerParams(
            dimension_semantics=("arbitrary",),
            vmem_limit_bytes=56 * 1024 * 1024,
        ),
    )(rows, cols, pt, stiffness)


def _dft_kernel(w_ref, x_ref, o_ref):
    x = x_ref[...]
    xh = x.astype(jnp.bfloat16)
    xl = (x - xh.astype(jnp.float32)).astype(jnp.bfloat16)
    w = w_ref[...]
    wh = w.astype(jnp.bfloat16)
    wl = (w - wh.astype(jnp.float32)).astype(jnp.bfloat16)
    acc = jnp.dot(wh, xh, preferred_element_type=jnp.float32)
    acc += jnp.dot(wh, xl, preferred_element_type=jnp.float32)
    acc += jnp.dot(wl, xh, preferred_element_type=jnp.float32)
    o_ref[...] = acc


def _dft(weights, x):
    rows, k = weights.shape
    n = x.shape[1]
    tn = 2048 if n % 2048 == 0 else n
    return pl.pallas_call(
        _dft_kernel,
        grid=(n // tn,),
        in_specs=[
            pl.BlockSpec((rows, k), lambda i: (0, 0)),
            pl.BlockSpec((k, tn), lambda i: (0, i)),
        ],
        out_specs=pl.BlockSpec((rows, tn), lambda i: (0, i)),
        out_shape=jax.ShapeDtypeStruct((rows, n), jnp.float32),
        compiler_params=pltpu.CompilerParams(dimension_semantics=("arbitrary",)),
    )(weights, x)


def _trig(h, b, count):
    angle = ((h * b) % count).astype(jnp.float32) * (2.0 * math.pi / count)
    return jnp.cos(angle), -jnp.sin(angle)


def body(panel, stiffness, block_rows, block_cols):
    nbl, nblk, bs, _ = stiffness.shape
    modes = panel.shape[-1]
    nbd = lax.axis_size("blade")
    mine = jnp.swapaxes(panel.reshape(-1, bs, modes), 1, 2)
    pt = lax.all_gather(mine, ("blade", "dof"), axis=0, tiled=True)
    proj = _project(pt, stiffness, block_rows.reshape(-1), block_cols.reshape(-1))

    half = lax.psum_scatter(proj, "dof", scatter_dimension=1, tiled=True)
    me = lax.axis_index("blade")
    rows_half = half.shape[1]
    r = rows_half // nbd
    chunks = half.reshape(nbl, nbd, r, modes)

    got = []
    for s in range(nbd):
        piece = lax.dynamic_index_in_dim(chunks, (me + s) % nbd, axis=1, keepdims=False)
        if s:
            piece = lax.ppermute(piece, "blade", [(j, (j + s) % nbd) for j in range(nbd)])
        got.append(piece)
    stacked = jnp.stack(got).reshape(nbd * nbl, r * modes)

    count = nbl * nbd
    src = (me - jnp.arange(nbd, dtype=jnp.int32)) % nbd
    blade = (nbl * src[:, None] + jnp.arange(nbl, dtype=jnp.int32)[None, :]).reshape(-1)
    dst = (me + jnp.arange(nbd, dtype=jnp.int32)) % nbd
    harm = (nbl * dst[:, None] + jnp.arange(nbl, dtype=jnp.int32)[None, :]).reshape(-1)
    cosine, sine = _trig(harm[:, None], blade[None, :], count)
    weights = jnp.stack([cosine.reshape(nbd, nbl, -1), sine.reshape(nbd, nbl, -1)], axis=1)
    spec = _dft(weights.reshape(2 * count, count), stacked)
    spec = spec.reshape(nbd, 2, nbl, r, modes)

    out = jnp.zeros((2, nbl, rows_half, modes), jnp.float32)
    for t in range(nbd):
        piece = spec[t]
        if t:
            piece = piece.astype(jnp.bfloat16)
            piece = lax.ppermute(piece, "blade", [(j, (j + t) % nbd) for j in range(nbd)])
            piece = piece.astype(jnp.float32)
        at = ((me - t) % nbd) * r
        out = lax.dynamic_update_slice(out, piece, (0, 0, at, 0))
    return out


def solution(mesh):
    placed = (
        P(("grp", "blade", "dof"), None),
        P(("grp", "blade"), "dof", None, None),
        P(("grp", "blade"), "dof"),
        P(("grp", "blade"), "dof"),
    )
    return jax.shard_map(
        body,
        mesh=mesh,
        in_specs=placed,
        out_specs=P(None, ("grp", "blade"), "dof", None),
        check_vma=False,
    )
```

```python
import math

import jax
import jax.numpy as jnp
from jax import lax
from jax.experimental import pallas as pl
from jax.experimental.pallas import tpu as pltpu
from jax.sharding import PartitionSpec as P


_NT = (((1,), (1,)), ((), ()))


def _project_kernel(rows_ref, cols_ref, pt_ref, s_ref, o_ref, lt_ref, it_ref):
    b = pl.program_id(0)
    nblk = s_ref.shape[1]
    bs = s_ref.shape[2]
    last = pt_ref.shape[0] - 1
    for n in range(nblk):
        c = jnp.minimum(jnp.maximum(cols_ref[b * nblk + n], 0), last)
        r = jnp.minimum(jnp.maximum(rows_ref[b * nblk + n], 0), last)
        im = lax.dot_general(pt_ref[c], s_ref[0, n], _NT, preferred_element_type=jnp.float32)
        it_ref[:, n * bs:(n + 1) * bs] = im.astype(jnp.bfloat16)
        lt_ref[:, n * bs:(n + 1) * bs] = pt_ref[r]
    o_ref[0] = lax.dot_general(lt_ref[...], it_ref[...], _NT, preferred_element_type=jnp.float32)


def _project(pt, stiffness, rows, cols):
    nbl, nblk, bs, _ = stiffness.shape
    nrb, modes, _ = pt.shape
    grid_spec = pltpu.PrefetchScalarGridSpec(
        num_scalar_prefetch=2,
        grid=(nbl,),
        in_specs=[
            pl.BlockSpec((nrb, modes, bs), lambda b, rr, cc: (0, 0, 0)),
            pl.BlockSpec((1, nblk, bs, bs), lambda b, rr, cc: (b, 0, 0, 0)),
        ],
        out_specs=pl.BlockSpec((1, modes, modes), lambda b, rr, cc: (b, 0, 0)),
        scratch_shapes=[
            pltpu.VMEM((modes, nblk * bs), jnp.bfloat16),
            pltpu.VMEM((modes, nblk * bs), jnp.bfloat16),
        ],
    )
    return pl.pallas_call(
        _project_kernel,
        grid_spec=grid_spec,
        out_shape=jax.ShapeDtypeStruct((nbl, modes, modes), jnp.float32),
        compiler_params=pltpu.CompilerParams(
            dimension_semantics=("arbitrary",),
            vmem_limit_bytes=56 * 1024 * 1024,
        ),
    )(rows, cols, pt, stiffness)


def _dft_kernel(w_ref, x_ref, o_ref):
    x = x_ref[...]
    xh = x.astype(jnp.bfloat16)
    xl = (x - xh.astype(jnp.float32)).astype(jnp.bfloat16)
    w = w_ref[...]
    wh = w.astype(jnp.bfloat16)
    wl = (w - wh.astype(jnp.float32)).astype(jnp.bfloat16)
    acc = jnp.dot(wh, xh, preferred_element_type=jnp.float32)
    acc += jnp.dot(wh, xl, preferred_element_type=jnp.float32)
    acc += jnp.dot(wl, xh, preferred_element_type=jnp.float32)
    o_ref[...] = acc.astype(o_ref.dtype)


def _dft(weights, x):
    rows, k = weights.shape
    n = x.shape[1]
    tn = 2048 if n % 2048 == 0 else n
    return pl.pallas_call(
        _dft_kernel,
        grid=(n // tn,),
        in_specs=[
            pl.BlockSpec((rows, k), lambda i: (0, 0)),
            pl.BlockSpec((k, tn), lambda i: (0, i)),
        ],
        out_specs=pl.BlockSpec((rows, tn), lambda i: (0, i)),
        out_shape=jax.ShapeDtypeStruct((rows, n), jnp.bfloat16),
        compiler_params=pltpu.CompilerParams(dimension_semantics=("arbitrary",)),
    )(weights, x)


def _trig(h, b, count):
    angle = ((h * b) % count).astype(jnp.float32) * (2.0 * math.pi / count)
    return jnp.cos(angle), -jnp.sin(angle)


def body(panel, stiffness, block_rows, block_cols):
    nbl, nblk, bs, _ = stiffness.shape
    modes = panel.shape[-1]
    nbd = lax.axis_size("blade")
    mine = jnp.swapaxes(panel.reshape(-1, bs, modes), 1, 2)
    pt = lax.all_gather(mine, ("blade", "dof"), axis=0, tiled=True)
    proj = _project(pt, stiffness, block_rows.reshape(-1), block_cols.reshape(-1))

    half = lax.psum_scatter(proj, "dof", scatter_dimension=1, tiled=True)
    me = lax.axis_index("blade")
    rows_half = half.shape[1]
    r = rows_half // nbd
    chunks = half.reshape(nbl, nbd, r, modes)

    got = []
    for s in range(nbd):
        piece = lax.dynamic_index_in_dim(chunks, (me + s) % nbd, axis=1, keepdims=False)
        if s:
            piece = lax.ppermute(piece, "blade", [(j, (j + s) % nbd) for j in range(nbd)])
        got.append(piece)
    stacked = jnp.stack(got).reshape(nbd * nbl, r * modes)

    count = nbl * nbd
    src = (me - jnp.arange(nbd, dtype=jnp.int32)) % nbd
    blade = (nbl * src[:, None] + jnp.arange(nbl, dtype=jnp.int32)[None, :]).reshape(-1)
    dst = (me + jnp.arange(nbd, dtype=jnp.int32)) % nbd
    harm = (nbl * dst[:, None] + jnp.arange(nbl, dtype=jnp.int32)[None, :]).reshape(-1)
    cosine, sine = _trig(harm[:, None], blade[None, :], count)
    weights = jnp.stack([cosine.reshape(nbd, nbl, -1), sine.reshape(nbd, nbl, -1)], axis=1)
    spec = _dft(weights.reshape(2 * count, count), stacked)
    spec = spec.reshape(nbd, 2, nbl, r, modes)

    out = jnp.zeros((2, nbl, rows_half, modes), jnp.float32)
    for t in range(nbd):
        piece = spec[t]
        if t:
            piece = lax.ppermute(piece, "blade", [(j, (j + t) % nbd) for j in range(nbd)])
        piece = piece.astype(jnp.float32)
        at = ((me - t) % nbd) * r
        out = lax.dynamic_update_slice(out, piece, (0, 0, at, 0))
    return out


def solution(mesh):
    placed = (
        P(("grp", "blade", "dof"), None),
        P(("grp", "blade"), "dof", None, None),
        P(("grp", "blade"), "dof"),
        P(("grp", "blade"), "dof"),
    )
    return jax.shard_map(
        body,
        mesh=mesh,
        in_specs=placed,
        out_specs=P(None, ("grp", "blade"), "dof", None),
        check_vma=False,
    )
```

```python
import math

import jax
import jax.numpy as jnp
from jax import lax
from jax.experimental import pallas as pl
from jax.experimental.pallas import tpu as pltpu
from jax.sharding import PartitionSpec as P


_NT = (((1,), (1,)), ((), ()))


def _project_kernel(rows_ref, cols_ref, pt_ref, s_ref, o_ref, lt_ref, it_ref):
    b = pl.program_id(0)
    nblk = s_ref.shape[1]
    bs = s_ref.shape[2]
    last = pt_ref.shape[0] - 1
    for n in range(nblk):
        c = jnp.minimum(jnp.maximum(cols_ref[b * nblk + n], 0), last)
        r = jnp.minimum(jnp.maximum(rows_ref[b * nblk + n], 0), last)
        im = lax.dot_general(pt_ref[c], s_ref[0, n], _NT, preferred_element_type=jnp.float32)
        it_ref[:, n * bs:(n + 1) * bs] = im.astype(jnp.bfloat16)
        lt_ref[:, n * bs:(n + 1) * bs] = pt_ref[r]
    o_ref[0] = lax.dot_general(lt_ref[...], it_ref[...], _NT, preferred_element_type=jnp.float32)


def _project(pt, stiffness, rows, cols):
    nbl, nblk, bs, _ = stiffness.shape
    nrb, modes, _ = pt.shape
    grid_spec = pltpu.PrefetchScalarGridSpec(
        num_scalar_prefetch=2,
        grid=(nbl,),
        in_specs=[
            pl.BlockSpec((nrb, modes, bs), lambda b, rr, cc: (0, 0, 0)),
            pl.BlockSpec((1, nblk, bs, bs), lambda b, rr, cc: (b, 0, 0, 0)),
        ],
        out_specs=pl.BlockSpec((1, modes, modes), lambda b, rr, cc: (b, 0, 0)),
        scratch_shapes=[
            pltpu.VMEM((modes, nblk * bs), jnp.bfloat16),
            pltpu.VMEM((modes, nblk * bs), jnp.bfloat16),
        ],
    )
    return pl.pallas_call(
        _project_kernel,
        grid_spec=grid_spec,
        out_shape=jax.ShapeDtypeStruct((nbl, modes, modes), jnp.float32),
        compiler_params=pltpu.CompilerParams(
            dimension_semantics=("arbitrary",),
            vmem_limit_bytes=56 * 1024 * 1024,
        ),
    )(rows, cols, pt, stiffness)


def _dft_kernel(w_ref, x_ref, o_ref):
    x = x_ref[...]
    xh = x.astype(jnp.bfloat16)
    xl = (x - xh.astype(jnp.float32)).astype(jnp.bfloat16)
    w = w_ref[...]
    wh = w.astype(jnp.bfloat16)
    wl = (w - wh.astype(jnp.float32)).astype(jnp.bfloat16)
    acc = jnp.dot(wh, xh, preferred_element_type=jnp.float32)
    acc += jnp.dot(wh, xl, preferred_element_type=jnp.float32)
    acc += jnp.dot(wl, xh, preferred_element_type=jnp.float32)
    o_ref[...] = acc


def _dft(weights, x):
    rows, k = weights.shape
    n = x.shape[1]
    tn = 2048 if n % 2048 == 0 else n
    return pl.pallas_call(
        _dft_kernel,
        grid=(n // tn,),
        in_specs=[
            pl.BlockSpec((rows, k), lambda i: (0, 0)),
            pl.BlockSpec((k, tn), lambda i: (0, i)),
        ],
        out_specs=pl.BlockSpec((rows, tn), lambda i: (0, i)),
        out_shape=jax.ShapeDtypeStruct((rows, n), jnp.float32),
        compiler_params=pltpu.CompilerParams(dimension_semantics=("arbitrary",)),
    )(weights, x)


def _trig(h, b, count):
    angle = ((h * b) % count).astype(jnp.float32) * (2.0 * math.pi / count)
    return jnp.cos(angle), -jnp.sin(angle)


def body(panel, stiffness, block_rows, block_cols):
    nbl, nblk, bs, _ = stiffness.shape
    modes = panel.shape[-1]
    nbd = lax.axis_size("blade")
    mine = jnp.swapaxes(panel.reshape(-1, bs, modes), 1, 2)
    pt = lax.all_gather(mine, ("blade", "dof"), axis=0, tiled=True)
    proj = _project(pt, stiffness, block_rows.reshape(-1), block_cols.reshape(-1))

    if lax.axis_size("dof") == 2:
        rows_half = modes // 2
        d = lax.axis_index("dof")
        mine = lax.dynamic_slice_in_dim(proj, d * rows_half, rows_half, axis=1)
        other = lax.dynamic_slice_in_dim(proj, (1 - d) * rows_half, rows_half, axis=1)
        half = mine + lax.ppermute(other, "dof", [(0, 1), (1, 0)])
    else:
        half = lax.psum_scatter(proj, "dof", scatter_dimension=1, tiled=True)
    me = lax.axis_index("blade")
    rows_half = half.shape[1]
    r = rows_half // nbd
    chunks = half.reshape(nbl, nbd, r, modes)

    got = []
    for s in range(nbd):
        piece = lax.dynamic_index_in_dim(chunks, (me + s) % nbd, axis=1, keepdims=False)
        if s:
            piece = lax.ppermute(piece, "blade", [(j, (j + s) % nbd) for j in range(nbd)])
        got.append(piece)
    stacked = jnp.stack(got).reshape(nbd * nbl, r * modes)

    count = nbl * nbd
    src = (me - jnp.arange(nbd, dtype=jnp.int32)) % nbd
    blade = (nbl * src[:, None] + jnp.arange(nbl, dtype=jnp.int32)[None, :]).reshape(-1)
    dst = (me + jnp.arange(nbd, dtype=jnp.int32)) % nbd
    harm = (nbl * dst[:, None] + jnp.arange(nbl, dtype=jnp.int32)[None, :]).reshape(-1)
    cosine, sine = _trig(harm[:, None], blade[None, :], count)
    weights = jnp.stack([cosine.reshape(nbd, nbl, -1), sine.reshape(nbd, nbl, -1)], axis=1)
    spec = _dft(weights.reshape(2 * count, count), stacked)
    spec = spec.reshape(nbd, 2, nbl, r, modes)

    out = jnp.zeros((2, nbl, rows_half, modes), jnp.float32)
    for t in range(nbd):
        piece = spec[t]
        if t:
            piece = piece.astype(jnp.bfloat16)
            piece = lax.ppermute(piece, "blade", [(j, (j + t) % nbd) for j in range(nbd)])
            piece = piece.astype(jnp.float32)
        at = ((me - t) % nbd) * r
        out = lax.dynamic_update_slice(out, piece, (0, 0, at, 0))
    return out


def solution(mesh):
    placed = (
        P(("grp", "blade", "dof"), None),
        P(("grp", "blade"), "dof", None, None),
        P(("grp", "blade"), "dof"),
        P(("grp", "blade"), "dof"),
    )
    return jax.shard_map(
        body,
        mesh=mesh,
        in_specs=placed,
        out_specs=P(None, ("grp", "blade"), "dof", None),
        check_vma=False,
    )
```

```python
import math

import jax
import jax.numpy as jnp
from jax import lax
from jax.experimental import pallas as pl
from jax.experimental.pallas import tpu as pltpu
from jax.sharding import PartitionSpec as P


_NT = (((1,), (1,)), ((), ()))


def _project_kernel(rows_ref, cols_ref, pt_ref, s_ref, o_ref, lt_ref, it_ref):
    b = pl.program_id(0)
    nblk = s_ref.shape[1]
    bs = s_ref.shape[2]
    last = pt_ref.shape[0] - 1
    for n in range(nblk):
        c = jnp.minimum(jnp.maximum(cols_ref[b * nblk + n], 0), last)
        r = jnp.minimum(jnp.maximum(rows_ref[b * nblk + n], 0), last)
        im = lax.dot_general(pt_ref[c], s_ref[0, n], _NT, preferred_element_type=jnp.float32)
        it_ref[:, n * bs:(n + 1) * bs] = im.astype(jnp.bfloat16)
        lt_ref[:, n * bs:(n + 1) * bs] = pt_ref[r]
    o_ref[0] = lax.dot_general(lt_ref[...], it_ref[...], _NT, preferred_element_type=jnp.float32)


def _project(pt, stiffness, rows, cols):
    nbl, nblk, bs, _ = stiffness.shape
    nrb, modes, _ = pt.shape
    grid_spec = pltpu.PrefetchScalarGridSpec(
        num_scalar_prefetch=2,
        grid=(nbl,),
        in_specs=[
            pl.BlockSpec((nrb, modes, bs), lambda b, rr, cc: (0, 0, 0)),
            pl.BlockSpec((1, nblk, bs, bs), lambda b, rr, cc: (b, 0, 0, 0)),
        ],
        out_specs=pl.BlockSpec((1, modes, modes), lambda b, rr, cc: (b, 0, 0)),
        scratch_shapes=[
            pltpu.VMEM((modes, nblk * bs), jnp.bfloat16),
            pltpu.VMEM((modes, nblk * bs), jnp.bfloat16),
        ],
    )
    return pl.pallas_call(
        _project_kernel,
        grid_spec=grid_spec,
        out_shape=jax.ShapeDtypeStruct((nbl, modes, modes), jnp.float32),
        compiler_params=pltpu.CompilerParams(
            dimension_semantics=("arbitrary",),
            vmem_limit_bytes=56 * 1024 * 1024,
        ),
    )(rows, cols, pt, stiffness)


def _dft_kernel(w_ref, x_ref, o_ref):
    x = x_ref[...]
    xh = x.astype(jnp.bfloat16)
    xl = (x - xh.astype(jnp.float32)).astype(jnp.bfloat16)
    w = w_ref[...]
    wh = w.astype(jnp.bfloat16)
    wl = (w - wh.astype(jnp.float32)).astype(jnp.bfloat16)
    acc = jnp.dot(wh, xh, preferred_element_type=jnp.float32)
    acc += jnp.dot(wh, xl, preferred_element_type=jnp.float32)
    acc += jnp.dot(wl, xh, preferred_element_type=jnp.float32)
    o_ref[...] = acc


def _dft(weights, x):
    rows, k = weights.shape
    n = x.shape[1]
    tn = 2048 if n % 2048 == 0 else n
    return pl.pallas_call(
        _dft_kernel,
        grid=(n // tn,),
        in_specs=[
            pl.BlockSpec((rows, k), lambda i: (0, 0)),
            pl.BlockSpec((k, tn), lambda i: (0, i)),
        ],
        out_specs=pl.BlockSpec((rows, tn), lambda i: (0, i)),
        out_shape=jax.ShapeDtypeStruct((rows, n), jnp.float32),
        compiler_params=pltpu.CompilerParams(dimension_semantics=("arbitrary",)),
    )(weights, x)


def _trig(h, b, count):
    angle = ((h * b) % count).astype(jnp.float32) * (2.0 * math.pi / count)
    return jnp.cos(angle), -jnp.sin(angle)


def body(panel, stiffness, block_rows, block_cols):
    nbl, nblk, bs, _ = stiffness.shape
    modes = panel.shape[-1]
    nbd = lax.axis_size("blade")
    mine = jnp.swapaxes(panel.reshape(-1, bs, modes), 1, 2)
    nd = lax.axis_size("dof")
    pt = lax.all_gather(mine, ("dof", "blade"), axis=0, tiled=True)
    bpd = mine.shape[0]

    def remap(j):
        j = jnp.clip(j.reshape(-1), 0, pt.shape[0] - 1)
        k = j // bpd
        return ((k % nd) * nbd + k // nd) * bpd + j % bpd

    proj = _project(pt, stiffness, remap(block_rows), remap(block_cols))

    if lax.axis_size("dof") == 2:
        rows_half = modes // 2
        d = lax.axis_index("dof")
        mine = lax.dynamic_slice_in_dim(proj, d * rows_half, rows_half, axis=1)
        other = lax.dynamic_slice_in_dim(proj, (1 - d) * rows_half, rows_half, axis=1)
        half = mine + lax.ppermute(other, "dof", [(0, 1), (1, 0)])
    else:
        half = lax.psum_scatter(proj, "dof", scatter_dimension=1, tiled=True)
    me = lax.axis_index("blade")
    rows_half = half.shape[1]
    r = rows_half // nbd
    chunks = half.reshape(nbl, nbd, r, modes)

    got = []
    for s in range(nbd):
        piece = lax.dynamic_index_in_dim(chunks, (me + s) % nbd, axis=1, keepdims=False)
        if s:
            piece = lax.ppermute(piece, "blade", [(j, (j + s) % nbd) for j in range(nbd)])
        got.append(piece)
    stacked = jnp.stack(got).reshape(nbd * nbl, r * modes)

    count = nbl * nbd
    src = (me - jnp.arange(nbd, dtype=jnp.int32)) % nbd
    blade = (nbl * src[:, None] + jnp.arange(nbl, dtype=jnp.int32)[None, :]).reshape(-1)
    dst = (me + jnp.arange(nbd, dtype=jnp.int32)) % nbd
    harm = (nbl * dst[:, None] + jnp.arange(nbl, dtype=jnp.int32)[None, :]).reshape(-1)
    cosine, sine = _trig(harm[:, None], blade[None, :], count)
    weights = jnp.stack([cosine.reshape(nbd, nbl, -1), sine.reshape(nbd, nbl, -1)], axis=1)
    spec = _dft(weights.reshape(2 * count, count), stacked)
    spec = spec.reshape(nbd, 2, nbl, r, modes)

    out = jnp.zeros((2, nbl, rows_half, modes), jnp.float32)
    for t in range(nbd):
        piece = spec[t]
        if t:
            piece = piece.astype(jnp.bfloat16)
            piece = lax.ppermute(piece, "blade", [(j, (j + t) % nbd) for j in range(nbd)])
            piece = piece.astype(jnp.float32)
        at = ((me - t) % nbd) * r
        out = lax.dynamic_update_slice(out, piece, (0, 0, at, 0))
    return out


def solution(mesh):
    placed = (
        P(("grp", "blade", "dof"), None),
        P(("grp", "blade"), "dof", None, None),
        P(("grp", "blade"), "dof"),
        P(("grp", "blade"), "dof"),
    )
    return jax.shard_map(
        body,
        mesh=mesh,
        in_specs=placed,
        out_specs=P(None, ("grp", "blade"), "dof", None),
        check_vma=False,
    )
```

```python
import math

import jax
import jax.numpy as jnp
from jax import lax
from jax.experimental import pallas as pl
from jax.experimental.pallas import tpu as pltpu
from jax.sharding import PartitionSpec as P


_NT = (((1,), (1,)), ((), ()))


def _project_kernel(rows_ref, cols_ref, pt_ref, s_ref, o_ref, lt_ref, it_ref):
    b = pl.program_id(0)
    nblk = s_ref.shape[1]
    bs = s_ref.shape[2]
    last = pt_ref.shape[0] - 1
    for n in range(nblk):
        c = jnp.minimum(jnp.maximum(cols_ref[b * nblk + n], 0), last)
        r = jnp.minimum(jnp.maximum(rows_ref[b * nblk + n], 0), last)
        im = lax.dot_general(pt_ref[c], s_ref[0, n], _NT, preferred_element_type=jnp.float32)
        it_ref[:, n * bs:(n + 1) * bs] = im.astype(jnp.bfloat16)
        lt_ref[:, n * bs:(n + 1) * bs] = pt_ref[r]
    o_ref[0] = lax.dot_general(lt_ref[...], it_ref[...], _NT, preferred_element_type=jnp.float32)


def _project(pt, stiffness, rows, cols):
    nbl, nblk, bs, _ = stiffness.shape
    nrb, modes, _ = pt.shape
    grid_spec = pltpu.PrefetchScalarGridSpec(
        num_scalar_prefetch=2,
        grid=(nbl,),
        in_specs=[
            pl.BlockSpec((nrb, modes, bs), lambda b, rr, cc: (0, 0, 0)),
            pl.BlockSpec((1, nblk, bs, bs), lambda b, rr, cc: (b, 0, 0, 0)),
        ],
        out_specs=pl.BlockSpec((1, modes, modes), lambda b, rr, cc: (b, 0, 0)),
        scratch_shapes=[
            pltpu.VMEM((modes, nblk * bs), jnp.bfloat16),
            pltpu.VMEM((modes, nblk * bs), jnp.bfloat16),
        ],
    )
    return pl.pallas_call(
        _project_kernel,
        grid_spec=grid_spec,
        out_shape=jax.ShapeDtypeStruct((nbl, modes, modes), jnp.float32),
        compiler_params=pltpu.CompilerParams(
            dimension_semantics=("arbitrary",),
            vmem_limit_bytes=56 * 1024 * 1024,
        ),
    )(rows, cols, pt, stiffness)


def _dft_kernel(w_ref, x_ref, o_ref):
    x = x_ref[...]
    xh = x.astype(jnp.bfloat16)
    xl = (x - xh.astype(jnp.float32)).astype(jnp.bfloat16)
    w = w_ref[...]
    wh = w.astype(jnp.bfloat16)
    wl = (w - wh.astype(jnp.float32)).astype(jnp.bfloat16)
    acc = jnp.dot(wh, xh, preferred_element_type=jnp.float32)
    acc += jnp.dot(wh, xl, preferred_element_type=jnp.float32)
    acc += jnp.dot(wl, xh, preferred_element_type=jnp.float32)
    o_ref[...] = acc


def _dft(weights, x):
    rows, k = weights.shape
    n = x.shape[1]
    tn = 2048 if n % 2048 == 0 else n
    return pl.pallas_call(
        _dft_kernel,
        grid=(n // tn,),
        in_specs=[
            pl.BlockSpec((rows, k), lambda i: (0, 0)),
            pl.BlockSpec((k, tn), lambda i: (0, i)),
        ],
        out_specs=pl.BlockSpec((rows, tn), lambda i: (0, i)),
        out_shape=jax.ShapeDtypeStruct((rows, n), jnp.float32),
        compiler_params=pltpu.CompilerParams(dimension_semantics=("arbitrary",)),
    )(weights, x)


def _trig(h, b, count):
    angle = ((h * b) % count).astype(jnp.float32) * (2.0 * math.pi / count)
    return jnp.cos(angle), -jnp.sin(angle)


def body(panel, stiffness, block_rows, block_cols):
    nbl, nblk, bs, _ = stiffness.shape
    modes = panel.shape[-1]
    nbd = lax.axis_size("blade")
    mine = jnp.swapaxes(panel.reshape(-1, bs, modes), 1, 2)
    pt = lax.all_gather(mine, ("blade", "dof"), axis=0, tiled=True)
    proj = _project(pt, stiffness, block_rows.reshape(-1), block_cols.reshape(-1))

    me = lax.axis_index("blade")
    rows_half = modes // lax.axis_size("dof")
    r = rows_half // nbd
    if lax.axis_size("dof") == 2:
        d = lax.axis_index("dof")
        mine = lax.dynamic_slice_in_dim(proj, d * rows_half, rows_half, axis=1)
        other = lax.dynamic_slice_in_dim(proj, (1 - d) * rows_half, rows_half, axis=1)
        halves = [mine, lax.ppermute(other, "dof", [(0, 1), (1, 0)])]
    else:
        halves = [lax.psum_scatter(proj, "dof", scatter_dimension=1, tiled=True)]
    halves = [h.reshape(nbl, nbd, r, modes) for h in halves]

    got = []
    for s in range(nbd):
        cut = [lax.dynamic_index_in_dim(h, (me + s) % nbd, axis=1, keepdims=False) for h in halves]
        piece = cut[0] + cut[1] if len(cut) > 1 else cut[0]
        if s:
            piece = lax.ppermute(piece, "blade", [(j, (j + s) % nbd) for j in range(nbd)])
        got.append(piece)
    stacked = jnp.stack(got).reshape(nbd * nbl, r * modes)

    count = nbl * nbd
    src = (me - jnp.arange(nbd, dtype=jnp.int32)) % nbd
    blade = (nbl * src[:, None] + jnp.arange(nbl, dtype=jnp.int32)[None, :]).reshape(-1)
    dst = (me + jnp.arange(nbd, dtype=jnp.int32)) % nbd
    harm = (nbl * dst[:, None] + jnp.arange(nbl, dtype=jnp.int32)[None, :]).reshape(-1)
    cosine, sine = _trig(harm[:, None], blade[None, :], count)
    weights = jnp.stack([cosine.reshape(nbd, nbl, -1), sine.reshape(nbd, nbl, -1)], axis=1)
    spec = _dft(weights.reshape(2 * count, count), stacked)
    spec = spec.reshape(nbd, 2, nbl, r, modes)

    out = jnp.zeros((2, nbl, rows_half, modes), jnp.float32)
    for t in range(nbd):
        piece = spec[t]
        if t:
            piece = piece.astype(jnp.bfloat16)
            piece = lax.ppermute(piece, "blade", [(j, (j + t) % nbd) for j in range(nbd)])
            piece = piece.astype(jnp.float32)
        at = ((me - t) % nbd) * r
        out = lax.dynamic_update_slice(out, piece, (0, 0, at, 0))
    return out


def solution(mesh):
    placed = (
        P(("grp", "blade", "dof"), None),
        P(("grp", "blade"), "dof", None, None),
        P(("grp", "blade"), "dof"),
        P(("grp", "blade"), "dof"),
    )
    return jax.shard_map(
        body,
        mesh=mesh,
        in_specs=placed,
        out_specs=P(None, ("grp", "blade"), "dof", None),
        check_vma=False,
    )
```

```python
import math

import jax
import jax.numpy as jnp
from jax import lax
from jax.experimental import pallas as pl
from jax.experimental.pallas import tpu as pltpu
from jax.sharding import PartitionSpec as P


_NT = (((1,), (1,)), ((), ()))


def _project_kernel(rows_ref, cols_ref, pt_ref, s_ref, o_ref, lt_ref, it_ref):
    b = pl.program_id(0)
    nblk = s_ref.shape[1]
    bs = s_ref.shape[2]
    last = pt_ref.shape[0] - 1
    for n in range(nblk):
        c = jnp.minimum(jnp.maximum(cols_ref[b * nblk + n], 0), last)
        r = jnp.minimum(jnp.maximum(rows_ref[b * nblk + n], 0), last)
        im = lax.dot_general(pt_ref[c], s_ref[0, n], _NT, preferred_element_type=jnp.float32)
        it_ref[:, n * bs:(n + 1) * bs] = im.astype(jnp.bfloat16)
        lt_ref[:, n * bs:(n + 1) * bs] = pt_ref[r]
    o_ref[0] = lax.dot_general(lt_ref[...], it_ref[...], _NT, preferred_element_type=jnp.float32)


def _project(pt, stiffness, rows, cols, start, nbl):
    _, nblk, bs, _ = stiffness.shape
    nrb, modes, _ = pt.shape
    rows = rows[start * nblk:(start + nbl) * nblk]
    cols = cols[start * nblk:(start + nbl) * nblk]
    grid_spec = pltpu.PrefetchScalarGridSpec(
        num_scalar_prefetch=2,
        grid=(nbl,),
        in_specs=[
            pl.BlockSpec((nrb, modes, bs), lambda b, rr, cc: (0, 0, 0)),
            pl.BlockSpec((1, nblk, bs, bs), lambda b, rr, cc: (b + start, 0, 0, 0)),
        ],
        out_specs=pl.BlockSpec((1, modes, modes), lambda b, rr, cc: (b, 0, 0)),
        scratch_shapes=[
            pltpu.VMEM((modes, nblk * bs), jnp.bfloat16),
            pltpu.VMEM((modes, nblk * bs), jnp.bfloat16),
        ],
    )
    return pl.pallas_call(
        _project_kernel,
        grid_spec=grid_spec,
        out_shape=jax.ShapeDtypeStruct((nbl, modes, modes), jnp.float32),
        compiler_params=pltpu.CompilerParams(
            dimension_semantics=("arbitrary",),
            vmem_limit_bytes=56 * 1024 * 1024,
        ),
    )(rows, cols, pt, stiffness)


def _dft_kernel(w_ref, x_ref, o_ref):
    x = x_ref[...]
    xh = x.astype(jnp.bfloat16)
    xl = (x - xh.astype(jnp.float32)).astype(jnp.bfloat16)
    w = w_ref[...]
    wh = w.astype(jnp.bfloat16)
    wl = (w - wh.astype(jnp.float32)).astype(jnp.bfloat16)
    acc = jnp.dot(wh, xh, preferred_element_type=jnp.float32)
    acc += jnp.dot(wh, xl, preferred_element_type=jnp.float32)
    acc += jnp.dot(wl, xh, preferred_element_type=jnp.float32)
    o_ref[...] = acc


def _dft(weights, x):
    rows, k = weights.shape
    n = x.shape[1]
    tn = 2048 if n % 2048 == 0 else n
    return pl.pallas_call(
        _dft_kernel,
        grid=(n // tn,),
        in_specs=[
            pl.BlockSpec((rows, k), lambda i: (0, 0)),
            pl.BlockSpec((k, tn), lambda i: (0, i)),
        ],
        out_specs=pl.BlockSpec((rows, tn), lambda i: (0, i)),
        out_shape=jax.ShapeDtypeStruct((rows, n), jnp.float32),
        compiler_params=pltpu.CompilerParams(dimension_semantics=("arbitrary",)),
    )(weights, x)


def _trig(h, b, count):
    angle = ((h * b) % count).astype(jnp.float32) * (2.0 * math.pi / count)
    return jnp.cos(angle), -jnp.sin(angle)


def body(panel, stiffness, block_rows, block_cols):
    nbl, nblk, bs, _ = stiffness.shape
    modes = panel.shape[-1]
    nbd = lax.axis_size("blade")
    mine = jnp.swapaxes(panel.reshape(-1, bs, modes), 1, 2)
    pt = lax.all_gather(mine, ("blade", "dof"), axis=0, tiled=True)
    rows_all = block_rows.reshape(-1)
    cols_all = block_cols.reshape(-1)
    me = lax.axis_index("blade")
    rows_half = modes // lax.axis_size("dof")
    r = rows_half // nbd

    groups = 2 if nbl % 2 == 0 else 1
    size = nbl // groups
    parts = [[] for _ in range(nbd)]
    for g in range(groups):
        proj = _project(pt, stiffness, rows_all, cols_all, g * size, size)
        if lax.axis_size("dof") == 2:
            d = lax.axis_index("dof")
            mine = lax.dynamic_slice_in_dim(proj, d * rows_half, rows_half, axis=1)
            other = lax.dynamic_slice_in_dim(proj, (1 - d) * rows_half, rows_half, axis=1)
            half = mine + lax.ppermute(other, "dof", [(0, 1), (1, 0)])
        else:
            half = lax.psum_scatter(proj, "dof", scatter_dimension=1, tiled=True)
        chunks = half.reshape(size, nbd, r, modes)
        for s in range(nbd):
            piece = lax.dynamic_index_in_dim(chunks, (me + s) % nbd, axis=1, keepdims=False)
            if s:
                piece = lax.ppermute(piece, "blade", [(j, (j + s) % nbd) for j in range(nbd)])
            parts[s].append(piece)
    got = [jnp.concatenate(p, axis=0) if len(p) > 1 else p[0] for p in parts]
    stacked = jnp.stack(got).reshape(nbd * nbl, r * modes)

    count = nbl * nbd
    src = (me - jnp.arange(nbd, dtype=jnp.int32)) % nbd
    blade = (nbl * src[:, None] + jnp.arange(nbl, dtype=jnp.int32)[None, :]).reshape(-1)
    dst = (me + jnp.arange(nbd, dtype=jnp.int32)) % nbd
    harm = (nbl * dst[:, None] + jnp.arange(nbl, dtype=jnp.int32)[None, :]).reshape(-1)
    cosine, sine = _trig(harm[:, None], blade[None, :], count)
    weights = jnp.stack([cosine.reshape(nbd, nbl, -1), sine.reshape(nbd, nbl, -1)], axis=1)
    spec = _dft(weights.reshape(2 * count, count), stacked)
    spec = spec.reshape(nbd, 2, nbl, r, modes)

    out = jnp.zeros((2, nbl, rows_half, modes), jnp.float32)
    for t in range(nbd):
        piece = spec[t]
        if t:
            piece = piece.astype(jnp.bfloat16)
            piece = lax.ppermute(piece, "blade", [(j, (j + t) % nbd) for j in range(nbd)])
            piece = piece.astype(jnp.float32)
        at = ((me - t) % nbd) * r
        out = lax.dynamic_update_slice(out, piece, (0, 0, at, 0))
    return out


def solution(mesh):
    placed = (
        P(("grp", "blade", "dof"), None),
        P(("grp", "blade"), "dof", None, None),
        P(("grp", "blade"), "dof"),
        P(("grp", "blade"), "dof"),
    )
    return jax.shard_map(
        body,
        mesh=mesh,
        in_specs=placed,
        out_specs=P(None, ("grp", "blade"), "dof", None),
        check_vma=False,
    )
```

```python
import math

import jax
import jax.numpy as jnp
from jax import lax
from jax.experimental import pallas as pl
from jax.experimental.pallas import tpu as pltpu
from jax.sharding import PartitionSpec as P


_NT = (((1,), (1,)), ((), ()))


def _project_kernel(rows_ref, cols_ref, pt_ref, s_ref, o_ref, lt_ref, it_ref):
    b = pl.program_id(0)
    nblk = s_ref.shape[1]
    bs = s_ref.shape[2]
    last = pt_ref.shape[0] - 1
    for n in range(nblk):
        c = jnp.minimum(jnp.maximum(cols_ref[b * nblk + n], 0), last)
        r = jnp.minimum(jnp.maximum(rows_ref[b * nblk + n], 0), last)
        im = lax.dot_general(pt_ref[c], s_ref[0, n], _NT, preferred_element_type=jnp.float32)
        it_ref[:, n * bs:(n + 1) * bs] = im.astype(jnp.bfloat16)
        lt_ref[:, n * bs:(n + 1) * bs] = pt_ref[r]
    o_ref[0] = lax.dot_general(lt_ref[...], it_ref[...], _NT, preferred_element_type=jnp.float32)


def _project(pt, stiffness, rows, cols):
    nbl, nblk, bs, _ = stiffness.shape
    nrb, modes, _ = pt.shape
    grid_spec = pltpu.PrefetchScalarGridSpec(
        num_scalar_prefetch=2,
        grid=(nbl,),
        in_specs=[
            pl.BlockSpec((nrb, modes, bs), lambda b, rr, cc: (0, 0, 0)),
            pl.BlockSpec((1, nblk, bs, bs), lambda b, rr, cc: (b, 0, 0, 0)),
        ],
        out_specs=pl.BlockSpec((1, modes, modes), lambda b, rr, cc: (b, 0, 0)),
        scratch_shapes=[
            pltpu.VMEM((modes, nblk * bs), jnp.bfloat16),
            pltpu.VMEM((modes, nblk * bs), jnp.bfloat16),
        ],
    )
    return pl.pallas_call(
        _project_kernel,
        grid_spec=grid_spec,
        out_shape=jax.ShapeDtypeStruct((nbl, modes, modes), jnp.float32),
        compiler_params=pltpu.CompilerParams(
            dimension_semantics=("arbitrary",),
            vmem_limit_bytes=56 * 1024 * 1024,
        ),
    )(rows, cols, pt, stiffness)


def _dft_kernel(w_ref, x_ref, o_ref):
    x = x_ref[...]
    xh = x.astype(jnp.bfloat16)
    xl = (x - xh.astype(jnp.float32)).astype(jnp.bfloat16)
    w = w_ref[...]
    wh = w.astype(jnp.bfloat16)
    wl = (w - wh.astype(jnp.float32)).astype(jnp.bfloat16)
    acc = jnp.dot(wh, xh, preferred_element_type=jnp.float32)
    acc += jnp.dot(wh, xl, preferred_element_type=jnp.float32)
    acc += jnp.dot(wl, xh, preferred_element_type=jnp.float32)
    o_ref[...] = acc


def _dft(weights, x):
    rows, k = weights.shape
    n = x.shape[1]
    tn = 2048 if n % 2048 == 0 else n
    return pl.pallas_call(
        _dft_kernel,
        grid=(n // tn,),
        in_specs=[
            pl.BlockSpec((rows, k), lambda i: (0, 0)),
            pl.BlockSpec((k, tn), lambda i: (0, i)),
        ],
        out_specs=pl.BlockSpec((rows, tn), lambda i: (0, i)),
        out_shape=jax.ShapeDtypeStruct((rows, n), jnp.float32),
        compiler_params=pltpu.CompilerParams(dimension_semantics=("arbitrary",)),
    )(weights, x)


def _trig(h, b, count):
    angle = ((h * b) % count).astype(jnp.float32) * (2.0 * math.pi / count)
    return jnp.cos(angle), -jnp.sin(angle)


def body(panel, stiffness, block_rows, block_cols):
    nbl, nblk, bs, _ = stiffness.shape
    modes = panel.shape[-1]
    nbd = lax.axis_size("blade")
    mine = jnp.swapaxes(panel.reshape(-1, bs, modes), 1, 2)
    pt = lax.all_gather(mine, ("blade", "dof"), axis=0, tiled=True)
    proj = _project(pt, stiffness, block_rows.reshape(-1), block_cols.reshape(-1))

    if lax.axis_size("dof") == 2:
        rows_half = modes // 2
        d = lax.axis_index("dof")
        mine = lax.dynamic_slice_in_dim(proj, d * rows_half, rows_half, axis=1)
        other = lax.dynamic_slice_in_dim(proj, (1 - d) * rows_half, rows_half, axis=1)
        half = mine + lax.ppermute(other, "dof", [(0, 1), (1, 0)])
    else:
        half = lax.psum_scatter(proj, "dof", scatter_dimension=1, tiled=True)
    me = lax.axis_index("blade")
    rows_half = half.shape[1]
    r = rows_half // nbd
    chunks = half.reshape(nbl, nbd, r, modes)

    count = nbl * nbd
    src = (me - jnp.arange(nbd, dtype=jnp.int32)) % nbd
    blade = (nbl * src[:, None] + jnp.arange(nbl, dtype=jnp.int32)[None, :]).reshape(-1)
    dst = (me + jnp.arange(nbd, dtype=jnp.int32)) % nbd
    harm = (nbl * dst[:, None] + jnp.arange(nbl, dtype=jnp.int32)[None, :]).reshape(-1)
    cosine, sine = _trig(harm[:, None], blade[None, :], count)
    weights = jnp.stack([cosine.reshape(nbd, nbl, -1), sine.reshape(nbd, nbl, -1)], axis=1)
    weights = weights.reshape(2 * count, count)

    nh = 2 if r % 16 == 0 else 1
    rh = r // nh
    out = jnp.zeros((2, nbl, rows_half, modes), jnp.float32)
    for hh in range(nh):
        got = []
        for s in range(nbd):
            piece = lax.dynamic_index_in_dim(chunks, (me + s) % nbd, axis=1, keepdims=False)
            piece = piece[:, hh * rh:(hh + 1) * rh]
            if s:
                piece = lax.ppermute(piece, "blade", [(j, (j + s) % nbd) for j in range(nbd)])
            got.append(piece)
        stacked = jnp.stack(got).reshape(nbd * nbl, rh * modes)
        spec = _dft(weights, stacked).reshape(nbd, 2, nbl, rh, modes)
        for t in range(nbd):
            piece = spec[t]
            if t:
                piece = piece.astype(jnp.bfloat16)
                piece = lax.ppermute(piece, "blade", [(j, (j + t) % nbd) for j in range(nbd)])
                piece = piece.astype(jnp.float32)
            at = ((me - t) % nbd) * r + hh * rh
            out = lax.dynamic_update_slice(out, piece, (0, 0, at, 0))
    return out


def solution(mesh):
    placed = (
        P(("grp", "blade", "dof"), None),
        P(("grp", "blade"), "dof", None, None),
        P(("grp", "blade"), "dof"),
        P(("grp", "blade"), "dof"),
    )
    return jax.shard_map(
        body,
        mesh=mesh,
        in_specs=placed,
        out_specs=P(None, ("grp", "blade"), "dof", None),
        check_vma=False,
    )
```

```python
import math

import jax
import jax.numpy as jnp
from jax import lax
from jax.experimental import pallas as pl
from jax.experimental.pallas import tpu as pltpu
from jax.sharding import PartitionSpec as P


_NT = (((1,), (1,)), ((), ()))


def _project_kernel(rows_ref, cols_ref, side_ref, pt_ref, s_ref, mine_ref, other_ref, lt_ref, it_ref):
    b = pl.program_id(0)
    nblk = s_ref.shape[1]
    bs = s_ref.shape[2]
    last = pt_ref.shape[0] - 1
    for n in range(nblk):
        c = jnp.minimum(jnp.maximum(cols_ref[b * nblk + n], 0), last)
        r = jnp.minimum(jnp.maximum(rows_ref[b * nblk + n], 0), last)
        im = lax.dot_general(pt_ref[c], s_ref[0, n], _NT, preferred_element_type=jnp.float32)
        it_ref[:, n * bs:(n + 1) * bs] = im.astype(jnp.bfloat16)
        lt_ref[:, n * bs:(n + 1) * bs] = pt_ref[r]
    acc = lax.dot_general(lt_ref[...], it_ref[...], _NT, preferred_element_type=jnp.float32)
    h = mine_ref.shape[1]
    first = side_ref[0] == 0
    mine_ref[0] = jnp.where(first, acc[:h], acc[h:])
    other_ref[0] = jnp.where(first, acc[h:], acc[:h])


def _project(pt, stiffness, rows, cols, side):
    nbl, nblk, bs, _ = stiffness.shape
    nrb, modes, _ = pt.shape
    h = modes // 2
    grid_spec = pltpu.PrefetchScalarGridSpec(
        num_scalar_prefetch=3,
        grid=(nbl,),
        in_specs=[
            pl.BlockSpec((nrb, modes, bs), lambda b, rr, cc, sd: (0, 0, 0)),
            pl.BlockSpec((1, nblk, bs, bs), lambda b, rr, cc, sd: (b, 0, 0, 0)),
        ],
        out_specs=[
            pl.BlockSpec((1, h, modes), lambda b, rr, cc, sd: (b, 0, 0)),
            pl.BlockSpec((1, h, modes), lambda b, rr, cc, sd: (b, 0, 0)),
        ],
        scratch_shapes=[
            pltpu.VMEM((modes, nblk * bs), jnp.bfloat16),
            pltpu.VMEM((modes, nblk * bs), jnp.bfloat16),
        ],
    )
    return pl.pallas_call(
        _project_kernel,
        grid_spec=grid_spec,
        out_shape=[jax.ShapeDtypeStruct((nbl, h, modes), jnp.float32)] * 2,
        compiler_params=pltpu.CompilerParams(
            dimension_semantics=("arbitrary",),
            vmem_limit_bytes=56 * 1024 * 1024,
        ),
    )(rows, cols, side, pt, stiffness)


def _dft_kernel(w_ref, x_ref, o_ref):
    x = x_ref[...]
    xh = x.astype(jnp.bfloat16)
    xl = (x - xh.astype(jnp.float32)).astype(jnp.bfloat16)
    w = w_ref[...]
    wh = w.astype(jnp.bfloat16)
    wl = (w - wh.astype(jnp.float32)).astype(jnp.bfloat16)
    acc = jnp.dot(wh, xh, preferred_element_type=jnp.float32)
    acc += jnp.dot(wh, xl, preferred_element_type=jnp.float32)
    acc += jnp.dot(wl, xh, preferred_element_type=jnp.float32)
    o_ref[...] = acc


def _dft(weights, x):
    rows, k = weights.shape
    n = x.shape[1]
    tn = 2048 if n % 2048 == 0 else n
    return pl.pallas_call(
        _dft_kernel,
        grid=(n // tn,),
        in_specs=[
            pl.BlockSpec((rows, k), lambda i: (0, 0)),
            pl.BlockSpec((k, tn), lambda i: (0, i)),
        ],
        out_specs=pl.BlockSpec((rows, tn), lambda i: (0, i)),
        out_shape=jax.ShapeDtypeStruct((rows, n), jnp.float32),
        compiler_params=pltpu.CompilerParams(dimension_semantics=("arbitrary",)),
    )(weights, x)


def _trig(h, b, count):
    angle = ((h * b) % count).astype(jnp.float32) * (2.0 * math.pi / count)
    return jnp.cos(angle), -jnp.sin(angle)


def body(panel, stiffness, block_rows, block_cols):
    nbl, nblk, bs, _ = stiffness.shape
    modes = panel.shape[-1]
    nbd = lax.axis_size("blade")
    mine = jnp.swapaxes(panel.reshape(-1, bs, modes), 1, 2)
    pt = lax.all_gather(mine, ("blade", "dof"), axis=0, tiled=True)
    nd = lax.axis_size("dof")
    side = (lax.axis_index("dof") % 2).reshape(1).astype(jnp.int32)
    mine, other = _project(pt, stiffness, block_rows.reshape(-1), block_cols.reshape(-1), side)

    if nd == 2:
        half = mine + lax.ppermute(other, "dof", [(0, 1), (1, 0)])
    else:
        proj = jnp.concatenate([mine, other], axis=1)
        half = lax.psum_scatter(proj, "dof", scatter_dimension=1, tiled=True)
    me = lax.axis_index("blade")
    rows_half = half.shape[1]
    r = rows_half // nbd
    chunks = half.reshape(nbl, nbd, r, modes)

    got = []
    for s in range(nbd):
        piece = lax.dynamic_index_in_dim(chunks, (me + s) % nbd, axis=1, keepdims=False)
        if s:
            piece = lax.ppermute(piece, "blade", [(j, (j + s) % nbd) for j in range(nbd)])
        got.append(piece)
    stacked = jnp.stack(got).reshape(nbd * nbl, r * modes)

    count = nbl * nbd
    src = (me - jnp.arange(nbd, dtype=jnp.int32)) % nbd
    blade = (nbl * src[:, None] + jnp.arange(nbl, dtype=jnp.int32)[None, :]).reshape(-1)
    dst = (me + jnp.arange(nbd, dtype=jnp.int32)) % nbd
    harm = (nbl * dst[:, None] + jnp.arange(nbl, dtype=jnp.int32)[None, :]).reshape(-1)
    cosine, sine = _trig(harm[:, None], blade[None, :], count)
    weights = jnp.stack([cosine.reshape(nbd, nbl, -1), sine.reshape(nbd, nbl, -1)], axis=1)
    spec = _dft(weights.reshape(2 * count, count), stacked)
    spec = spec.reshape(nbd, 2, nbl, r, modes)

    out = jnp.zeros((2, nbl, rows_half, modes), jnp.float32)
    for t in range(nbd):
        piece = spec[t]
        if t:
            piece = piece.astype(jnp.bfloat16)
            piece = lax.ppermute(piece, "blade", [(j, (j + t) % nbd) for j in range(nbd)])
            piece = piece.astype(jnp.float32)
        at = ((me - t) % nbd) * r
        out = lax.dynamic_update_slice(out, piece, (0, 0, at, 0))
    return out


def solution(mesh):
    placed = (
        P(("grp", "blade", "dof"), None),
        P(("grp", "blade"), "dof", None, None),
        P(("grp", "blade"), "dof"),
        P(("grp", "blade"), "dof"),
    )
    return jax.shard_map(
        body,
        mesh=mesh,
        in_specs=placed,
        out_specs=P(None, ("grp", "blade"), "dof", None),
        check_vma=False,
    )
```

```python
import math

import jax
import jax.numpy as jnp
from jax import lax
from jax.experimental import pallas as pl
from jax.experimental.pallas import tpu as pltpu
from jax.sharding import PartitionSpec as P


_NT = (((1,), (1,)), ((), ()))


def _project_kernel(rows_ref, cols_ref, side_ref, pt_ref, s_ref, mine_ref, other_ref, lt_ref, it_ref):
    b = pl.program_id(0)
    nblk = s_ref.shape[1]
    bs = s_ref.shape[2]
    last = pt_ref.shape[0] - 1
    for n in range(nblk):
        c = jnp.minimum(jnp.maximum(cols_ref[b * nblk + n], 0), last)
        r = jnp.minimum(jnp.maximum(rows_ref[b * nblk + n], 0), last)
        im = lax.dot_general(pt_ref[c], s_ref[0, n], _NT, preferred_element_type=jnp.float32)
        it_ref[:, n * bs:(n + 1) * bs] = im.astype(jnp.bfloat16)
        lt_ref[:, n * bs:(n + 1) * bs] = pt_ref[r]
    acc = lax.dot_general(lt_ref[...], it_ref[...], _NT, preferred_element_type=jnp.float32)
    h = mine_ref.shape[1]
    first = side_ref[0] == 0
    mine_ref[0] = jnp.where(first, acc[:h], acc[h:])
    other_ref[0] = jnp.where(first, acc[h:], acc[:h])


def _project(pt, stiffness, rows, cols, side):
    nbl, nblk, bs, _ = stiffness.shape
    nrb, modes, _ = pt.shape
    h = modes // 2
    grid_spec = pltpu.PrefetchScalarGridSpec(
        num_scalar_prefetch=3,
        grid=(nbl,),
        in_specs=[
            pl.BlockSpec((nrb, modes, bs), lambda b, rr, cc, sd: (0, 0, 0)),
            pl.BlockSpec((1, nblk, bs, bs), lambda b, rr, cc, sd: (b, 0, 0, 0)),
        ],
        out_specs=[
            pl.BlockSpec((1, h, modes), lambda b, rr, cc, sd: (b, 0, 0)),
            pl.BlockSpec((1, h, modes), lambda b, rr, cc, sd: (b, 0, 0)),
        ],
        scratch_shapes=[
            pltpu.VMEM((modes, nblk * bs), jnp.bfloat16),
            pltpu.VMEM((modes, nblk * bs), jnp.bfloat16),
        ],
    )
    return pl.pallas_call(
        _project_kernel,
        grid_spec=grid_spec,
        out_shape=[jax.ShapeDtypeStruct((nbl, h, modes), jnp.float32)] * 2,
        compiler_params=pltpu.CompilerParams(
            dimension_semantics=("arbitrary",),
            vmem_limit_bytes=56 * 1024 * 1024,
        ),
    )(rows, cols, side, pt, stiffness)


def _dft_kernel(w_ref, x_ref, o_ref):
    x = x_ref[...]
    xh = x.astype(jnp.bfloat16)
    xl = (x - xh.astype(jnp.float32)).astype(jnp.bfloat16)
    w = w_ref[...]
    wh = w.astype(jnp.bfloat16)
    wl = (w - wh.astype(jnp.float32)).astype(jnp.bfloat16)
    acc = jnp.dot(wh, xh, preferred_element_type=jnp.float32)
    acc += jnp.dot(wh, xl, preferred_element_type=jnp.float32)
    acc += jnp.dot(wl, xh, preferred_element_type=jnp.float32)
    o_ref[...] = acc


def _dft(weights, x):
    rows, k = weights.shape
    n = x.shape[1]
    tn = 2048 if n % 2048 == 0 else n
    return pl.pallas_call(
        _dft_kernel,
        grid=(n // tn,),
        in_specs=[
            pl.BlockSpec((rows, k), lambda i: (0, 0)),
            pl.BlockSpec((k, tn), lambda i: (0, i)),
        ],
        out_specs=pl.BlockSpec((rows, tn), lambda i: (0, i)),
        out_shape=jax.ShapeDtypeStruct((rows, n), jnp.float32),
        compiler_params=pltpu.CompilerParams(dimension_semantics=("arbitrary",)),
    )(weights, x)


def _trig(h, b, count):
    angle = ((h * b) % count).astype(jnp.float32) * (2.0 * math.pi / count)
    return jnp.cos(angle), -jnp.sin(angle)


def _shift_order(n):
    rest = sorted(range(1, n), key=lambda s: -min(s, n - s))
    out = [0]
    while rest:
        out.append(rest.pop(0))
        if rest:
            out.append(rest.pop())
    return out


def body(panel, stiffness, block_rows, block_cols):
    nbl, nblk, bs, _ = stiffness.shape
    modes = panel.shape[-1]
    nbd = lax.axis_size("blade")
    mine = jnp.swapaxes(panel.reshape(-1, bs, modes), 1, 2)
    pt = lax.all_gather(mine, ("blade", "dof"), axis=0, tiled=True)
    nd = lax.axis_size("dof")
    side = (lax.axis_index("dof") % 2).reshape(1).astype(jnp.int32)
    mine, other = _project(pt, stiffness, block_rows.reshape(-1), block_cols.reshape(-1), side)

    if nd == 2:
        half = mine + lax.ppermute(other, "dof", [(0, 1), (1, 0)])
    else:
        proj = jnp.concatenate([mine, other], axis=1)
        half = lax.psum_scatter(proj, "dof", scatter_dimension=1, tiled=True)
    me = lax.axis_index("blade")
    rows_half = half.shape[1]
    r = rows_half // nbd
    chunks = half.reshape(nbl, nbd, r, modes)

    order = _shift_order(nbd)
    got = [None] * nbd
    for s in order:
        piece = lax.dynamic_index_in_dim(chunks, (me + s) % nbd, axis=1, keepdims=False)
        if s:
            piece = lax.ppermute(piece, "blade", [(j, (j + s) % nbd) for j in range(nbd)])
        got[s] = piece
    stacked = jnp.stack(got).reshape(nbd * nbl, r * modes)

    count = nbl * nbd
    src = (me - jnp.arange(nbd, dtype=jnp.int32)) % nbd
    blade = (nbl * src[:, None] + jnp.arange(nbl, dtype=jnp.int32)[None, :]).reshape(-1)
    dst = (me + jnp.arange(nbd, dtype=jnp.int32)) % nbd
    harm = (nbl * dst[:, None] + jnp.arange(nbl, dtype=jnp.int32)[None, :]).reshape(-1)
    cosine, sine = _trig(harm[:, None], blade[None, :], count)
    weights = jnp.stack([cosine.reshape(nbd, nbl, -1), sine.reshape(nbd, nbl, -1)], axis=1)
    spec = _dft(weights.reshape(2 * count, count), stacked)
    spec = spec.reshape(nbd, 2, nbl, r, modes)

    out = jnp.zeros((2, nbl, rows_half, modes), jnp.float32)
    for t in order:
        piece = spec[t]
        if t:
            piece = piece.astype(jnp.bfloat16)
            piece = lax.ppermute(piece, "blade", [(j, (j + t) % nbd) for j in range(nbd)])
            piece = piece.astype(jnp.float32)
        at = ((me - t) % nbd) * r
        out = lax.dynamic_update_slice(out, piece, (0, 0, at, 0))
    return out


def solution(mesh):
    placed = (
        P(("grp", "blade", "dof"), None),
        P(("grp", "blade"), "dof", None, None),
        P(("grp", "blade"), "dof"),
        P(("grp", "blade"), "dof"),
    )
    return jax.shard_map(
        body,
        mesh=mesh,
        in_specs=placed,
        out_specs=P(None, ("grp", "blade"), "dof", None),
        check_vma=False,
    )
```

```python
import math

import jax
import jax.numpy as jnp
from jax import lax
from jax.experimental import pallas as pl
from jax.experimental.pallas import tpu as pltpu
from jax.sharding import PartitionSpec as P


_NT = (((1,), (1,)), ((), ()))


def _project_kernel(rows_ref, cols_ref, side_ref, pt_ref, s_ref, mine_ref, other_ref, lt_ref, it_ref):
    b = pl.program_id(0)
    nblk = s_ref.shape[1]
    bs = s_ref.shape[2]
    last = pt_ref.shape[0] - 1
    for n in range(nblk):
        c = jnp.minimum(jnp.maximum(cols_ref[b * nblk + n], 0), last)
        r = jnp.minimum(jnp.maximum(rows_ref[b * nblk + n], 0), last)
        im = lax.dot_general(pt_ref[c], s_ref[0, n], _NT, preferred_element_type=jnp.float32)
        it_ref[:, n * bs:(n + 1) * bs] = im.astype(jnp.bfloat16)
        lt_ref[:, n * bs:(n + 1) * bs] = pt_ref[r]
    acc = lax.dot_general(lt_ref[...], it_ref[...], _NT, preferred_element_type=jnp.float32)
    h = mine_ref.shape[1]
    first = side_ref[0] == 0
    mine_ref[0] = jnp.where(first, acc[:h], acc[h:])
    other_ref[0] = jnp.where(first, acc[h:], acc[:h])


def _project(pt, stiffness, rows, cols, side):
    nbl, nblk, bs, _ = stiffness.shape
    nrb, modes, _ = pt.shape
    h = modes // 2
    grid_spec = pltpu.PrefetchScalarGridSpec(
        num_scalar_prefetch=3,
        grid=(nbl,),
        in_specs=[
            pl.BlockSpec((nrb, modes, bs), lambda b, rr, cc, sd: (0, 0, 0)),
            pl.BlockSpec((1, nblk, bs, bs), lambda b, rr, cc, sd: (b, 0, 0, 0)),
        ],
        out_specs=[
            pl.BlockSpec((1, h, modes), lambda b, rr, cc, sd: (b, 0, 0)),
            pl.BlockSpec((1, h, modes), lambda b, rr, cc, sd: (b, 0, 0)),
        ],
        scratch_shapes=[
            pltpu.VMEM((modes, nblk * bs), jnp.bfloat16),
            pltpu.VMEM((modes, nblk * bs), jnp.bfloat16),
        ],
    )
    return pl.pallas_call(
        _project_kernel,
        grid_spec=grid_spec,
        out_shape=[jax.ShapeDtypeStruct((nbl, h, modes), jnp.float32)] * 2,
        compiler_params=pltpu.CompilerParams(
            dimension_semantics=("arbitrary",),
            vmem_limit_bytes=56 * 1024 * 1024,
        ),
    )(rows, cols, side, pt, stiffness)


def _dft_kernel(w_ref, x_ref, own_ref, far_ref):
    x = x_ref[...]
    xh = x.astype(jnp.bfloat16)
    xl = (x - xh.astype(jnp.float32)).astype(jnp.bfloat16)
    w = w_ref[...]
    wh = w.astype(jnp.bfloat16)
    wl = (w - wh.astype(jnp.float32)).astype(jnp.bfloat16)
    acc = jnp.dot(wh, xh, preferred_element_type=jnp.float32)
    acc += jnp.dot(wh, xl, preferred_element_type=jnp.float32)
    acc += jnp.dot(wl, xh, preferred_element_type=jnp.float32)
    k = own_ref.shape[0]
    own_ref[...] = acc[:k]
    far_ref[...] = acc[k:].astype(far_ref.dtype)


def _dft(weights, x, own):
    rows, k = weights.shape
    n = x.shape[1]
    tn = 2048 if n % 2048 == 0 else n
    return pl.pallas_call(
        _dft_kernel,
        grid=(n // tn,),
        in_specs=[
            pl.BlockSpec((rows, k), lambda i: (0, 0)),
            pl.BlockSpec((k, tn), lambda i: (0, i)),
        ],
        out_specs=[
            pl.BlockSpec((own, tn), lambda i: (0, i)),
            pl.BlockSpec((rows - own, tn), lambda i: (0, i)),
        ],
        out_shape=[
            jax.ShapeDtypeStruct((own, n), jnp.float32),
            jax.ShapeDtypeStruct((rows - own, n), jnp.bfloat16),
        ],
        compiler_params=pltpu.CompilerParams(dimension_semantics=("arbitrary",)),
    )(weights, x)


def _trig(h, b, count):
    angle = ((h * b) % count).astype(jnp.float32) * (2.0 * math.pi / count)
    return jnp.cos(angle), -jnp.sin(angle)


def body(panel, stiffness, block_rows, block_cols):
    nbl, nblk, bs, _ = stiffness.shape
    modes = panel.shape[-1]
    nbd = lax.axis_size("blade")
    mine = jnp.swapaxes(panel.reshape(-1, bs, modes), 1, 2)
    pt = lax.all_gather(mine, ("blade", "dof"), axis=0, tiled=True)
    nd = lax.axis_size("dof")
    side = (lax.axis_index("dof") % 2).reshape(1).astype(jnp.int32)
    mine, other = _project(pt, stiffness, block_rows.reshape(-1), block_cols.reshape(-1), side)

    if nd == 2:
        half = mine + lax.ppermute(other, "dof", [(0, 1), (1, 0)])
    else:
        proj = jnp.concatenate([mine, other], axis=1)
        half = lax.psum_scatter(proj, "dof", scatter_dimension=1, tiled=True)
    me = lax.axis_index("blade")
    rows_half = half.shape[1]
    r = rows_half // nbd
    chunks = half.reshape(nbl, nbd, r, modes)

    got = []
    for s in range(nbd):
        piece = lax.dynamic_index_in_dim(chunks, (me + s) % nbd, axis=1, keepdims=False)
        if s:
            piece = lax.ppermute(piece, "blade", [(j, (j + s) % nbd) for j in range(nbd)])
        got.append(piece)
    stacked = jnp.stack(got).reshape(nbd * nbl, r * modes)

    count = nbl * nbd
    src = (me - jnp.arange(nbd, dtype=jnp.int32)) % nbd
    blade = (nbl * src[:, None] + jnp.arange(nbl, dtype=jnp.int32)[None, :]).reshape(-1)
    dst = (me + jnp.arange(nbd, dtype=jnp.int32)) % nbd
    harm = (nbl * dst[:, None] + jnp.arange(nbl, dtype=jnp.int32)[None, :]).reshape(-1)
    cosine, sine = _trig(harm[:, None], blade[None, :], count)
    weights = jnp.stack([cosine.reshape(nbd, nbl, -1), sine.reshape(nbd, nbl, -1)], axis=1)
    own, far = _dft(weights.reshape(2 * count, count), stacked, 2 * nbl)
    far = far.reshape(nbd - 1, 2, nbl, r, modes)

    out = jnp.zeros((2, nbl, rows_half, modes), jnp.float32)
    for t in range(nbd):
        if t:
            piece = far[t - 1]
            piece = lax.ppermute(piece, "blade", [(j, (j + t) % nbd) for j in range(nbd)])
            piece = piece.astype(jnp.float32)
        else:
            piece = own.reshape(2, nbl, r, modes)
        at = ((me - t) % nbd) * r
        out = lax.dynamic_update_slice(out, piece, (0, 0, at, 0))
    return out


def solution(mesh):
    placed = (
        P(("grp", "blade", "dof"), None),
        P(("grp", "blade"), "dof", None, None),
        P(("grp", "blade"), "dof"),
        P(("grp", "blade"), "dof"),
    )
    return jax.shard_map(
        body,
        mesh=mesh,
        in_specs=placed,
        out_specs=P(None, ("grp", "blade"), "dof", None),
        check_vma=False,
    )
```

```python
import math

import jax
import jax.numpy as jnp
from jax import lax
from jax.experimental import pallas as pl
from jax.experimental.pallas import tpu as pltpu
from jax.sharding import PartitionSpec as P


_NT = (((1,), (1,)), ((), ()))


def _project_kernel(rows_ref, cols_ref, side_ref, pt_ref, s_ref, mine_ref, other_ref, lt_ref, it_ref):
    b = pl.program_id(0)
    nblk = s_ref.shape[1]
    bs = s_ref.shape[2]
    last = pt_ref.shape[0] - 1
    for n in range(nblk):
        c = jnp.minimum(jnp.maximum(cols_ref[b * nblk + n], 0), last)
        r = jnp.minimum(jnp.maximum(rows_ref[b * nblk + n], 0), last)
        im = lax.dot_general(pt_ref[c], s_ref[0, n], _NT, preferred_element_type=jnp.float32)
        it_ref[:, n * bs:(n + 1) * bs] = im.astype(jnp.bfloat16)
        lt_ref[:, n * bs:(n + 1) * bs] = pt_ref[r]
    acc = lax.dot_general(lt_ref[...], it_ref[...], _NT, preferred_element_type=jnp.float32)
    h = mine_ref.shape[1]
    first = side_ref[0] == 0
    mine_ref[0] = jnp.where(first, acc[:h], acc[h:])
    other_ref[0] = jnp.where(first, acc[h:], acc[:h])


def _project(pt, stiffness, rows, cols, side):
    nbl, nblk, bs, _ = stiffness.shape
    nrb, modes, _ = pt.shape
    h = modes // 2
    grid_spec = pltpu.PrefetchScalarGridSpec(
        num_scalar_prefetch=3,
        grid=(nbl,),
        in_specs=[
            pl.BlockSpec((nrb, modes, bs), lambda b, rr, cc, sd: (0, 0, 0)),
            pl.BlockSpec((1, nblk, bs, bs), lambda b, rr, cc, sd: (b, 0, 0, 0)),
        ],
        out_specs=[
            pl.BlockSpec((1, h, modes), lambda b, rr, cc, sd: (b, 0, 0)),
            pl.BlockSpec((1, h, modes), lambda b, rr, cc, sd: (b, 0, 0)),
        ],
        scratch_shapes=[
            pltpu.VMEM((modes, nblk * bs), jnp.bfloat16),
            pltpu.VMEM((modes, nblk * bs), jnp.bfloat16),
        ],
    )
    return pl.pallas_call(
        _project_kernel,
        grid_spec=grid_spec,
        out_shape=[jax.ShapeDtypeStruct((nbl, h, modes), jnp.float32)] * 2,
        compiler_params=pltpu.CompilerParams(
            dimension_semantics=("arbitrary",),
            vmem_limit_bytes=56 * 1024 * 1024,
        ),
    )(rows, cols, side, pt, stiffness)


def _dft_kernel(w_ref, x_ref, own_ref, far_ref):
    x = x_ref[...]
    xh = x.astype(jnp.bfloat16)
    xl = (x - xh.astype(jnp.float32)).astype(jnp.bfloat16)
    w = w_ref[...]
    wh = w.astype(jnp.bfloat16)
    wl = (w - wh.astype(jnp.float32)).astype(jnp.bfloat16)
    acc = jnp.dot(wh, xh, preferred_element_type=jnp.float32)
    acc += jnp.dot(wh, xl, preferred_element_type=jnp.float32)
    acc += jnp.dot(wl, xh, preferred_element_type=jnp.float32)
    k = own_ref.shape[0]
    own_ref[...] = acc[:k]
    far_ref[...] = acc[k:].astype(far_ref.dtype)


def _dft(weights, x, own):
    rows, k = weights.shape
    n = x.shape[1]
    tn = 4096 if n % 4096 == 0 else n
    return pl.pallas_call(
        _dft_kernel,
        grid=(n // tn,),
        in_specs=[
            pl.BlockSpec((rows, k), lambda i: (0, 0)),
            pl.BlockSpec((k, tn), lambda i: (0, i)),
        ],
        out_specs=[
            pl.BlockSpec((own, tn), lambda i: (0, i)),
            pl.BlockSpec((rows - own, tn), lambda i: (0, i)),
        ],
        out_shape=[
            jax.ShapeDtypeStruct((own, n), jnp.float32),
            jax.ShapeDtypeStruct((rows - own, n), jnp.bfloat16),
        ],
        compiler_params=pltpu.CompilerParams(dimension_semantics=("arbitrary",)),
    )(weights, x)


def _trig(h, b, count):
    angle = ((h * b) % count).astype(jnp.float32) * (2.0 * math.pi / count)
    return jnp.cos(angle), -jnp.sin(angle)


def body(panel, stiffness, block_rows, block_cols):
    nbl, nblk, bs, _ = stiffness.shape
    modes = panel.shape[-1]
    nbd = lax.axis_size("blade")
    mine = jnp.swapaxes(panel.reshape(-1, bs, modes), 1, 2)
    pt = lax.all_gather(mine, ("blade", "dof"), axis=0, tiled=True)
    nd = lax.axis_size("dof")
    side = (lax.axis_index("dof") % 2).reshape(1).astype(jnp.int32)
    mine, other = _project(pt, stiffness, block_rows.reshape(-1), block_cols.reshape(-1), side)

    if nd == 2:
        half = mine + lax.ppermute(other, "dof", [(0, 1), (1, 0)])
    else:
        proj = jnp.concatenate([mine, other], axis=1)
        half = lax.psum_scatter(proj, "dof", scatter_dimension=1, tiled=True)
    me = lax.axis_index("blade")
    rows_half = half.shape[1]
    r = rows_half // nbd
    chunks = half.reshape(nbl, nbd, r, modes)

    got = []
    for s in range(nbd):
        piece = lax.dynamic_index_in_dim(chunks, (me + s) % nbd, axis=1, keepdims=False)
        if s:
            piece = lax.ppermute(piece, "blade", [(j, (j + s) % nbd) for j in range(nbd)])
        got.append(piece)
    stacked = jnp.stack(got).reshape(nbd * nbl, r * modes)

    count = nbl * nbd
    src = (me - jnp.arange(nbd, dtype=jnp.int32)) % nbd
    blade = (nbl * src[:, None] + jnp.arange(nbl, dtype=jnp.int32)[None, :]).reshape(-1)
    dst = (me + jnp.arange(nbd, dtype=jnp.int32)) % nbd
    harm = (nbl * dst[:, None] + jnp.arange(nbl, dtype=jnp.int32)[None, :]).reshape(-1)
    cosine, sine = _trig(harm[:, None], blade[None, :], count)
    weights = jnp.stack([cosine.reshape(nbd, nbl, -1), sine.reshape(nbd, nbl, -1)], axis=1)
    own, far = _dft(weights.reshape(2 * count, count), stacked, 2 * nbl)
    far = far.reshape(nbd - 1, 2, nbl, r, modes)

    out = jnp.zeros((2, nbl, rows_half, modes), jnp.float32)
    for t in range(nbd):
        if t:
            piece = far[t - 1]
            piece = lax.ppermute(piece, "blade", [(j, (j + t) % nbd) for j in range(nbd)])
            piece = piece.astype(jnp.float32)
        else:
            piece = own.reshape(2, nbl, r, modes)
        at = ((me - t) % nbd) * r
        out = lax.dynamic_update_slice(out, piece, (0, 0, at, 0))
    return out


def solution(mesh):
    placed = (
        P(("grp", "blade", "dof"), None),
        P(("grp", "blade"), "dof", None, None),
        P(("grp", "blade"), "dof"),
        P(("grp", "blade"), "dof"),
    )
    return jax.shard_map(
        body,
        mesh=mesh,
        in_specs=placed,
        out_specs=P(None, ("grp", "blade"), "dof", None),
        check_vma=False,
    )
```

```python
import math

import jax
import jax.numpy as jnp
from jax import lax
from jax.experimental import pallas as pl
from jax.experimental.pallas import tpu as pltpu
from jax.sharding import PartitionSpec as P


_NT = (((1,), (1,)), ((), ()))


def _project_kernel(rows_ref, cols_ref, side_ref, pt_ref, s_ref, mine_ref, other_ref, lt_ref, it_ref):
    b = pl.program_id(0)
    nblk = s_ref.shape[1]
    bs = s_ref.shape[2]
    last = pt_ref.shape[0] - 1
    for n in range(nblk):
        c = jnp.minimum(jnp.maximum(cols_ref[b * nblk + n], 0), last)
        r = jnp.minimum(jnp.maximum(rows_ref[b * nblk + n], 0), last)
        im = lax.dot_general(pt_ref[c], s_ref[0, n], _NT, preferred_element_type=jnp.float32)
        it_ref[:, n * bs:(n + 1) * bs] = im.astype(jnp.bfloat16)
        lt_ref[:, n * bs:(n + 1) * bs] = pt_ref[r]
    acc = lax.dot_general(lt_ref[...], it_ref[...], _NT, preferred_element_type=jnp.float32)
    h = mine_ref.shape[1]
    first = side_ref[0] == 0
    mine_ref[0] = jnp.where(first, acc[:h], acc[h:])
    other_ref[0] = jnp.where(first, acc[h:], acc[:h])


def _project(pt, stiffness, rows, cols, side):
    nbl, nblk, bs, _ = stiffness.shape
    nrb, modes, _ = pt.shape
    h = modes // 2
    grid_spec = pltpu.PrefetchScalarGridSpec(
        num_scalar_prefetch=3,
        grid=(nbl,),
        in_specs=[
            pl.BlockSpec((nrb, modes, bs), lambda b, rr, cc, sd: (0, 0, 0)),
            pl.BlockSpec((1, nblk, bs, bs), lambda b, rr, cc, sd: (b, 0, 0, 0)),
        ],
        out_specs=[
            pl.BlockSpec((1, h, modes), lambda b, rr, cc, sd: (b, 0, 0)),
            pl.BlockSpec((1, h, modes), lambda b, rr, cc, sd: (b, 0, 0)),
        ],
        scratch_shapes=[
            pltpu.VMEM((modes, nblk * bs), jnp.bfloat16),
            pltpu.VMEM((modes, nblk * bs), jnp.bfloat16),
        ],
    )
    return pl.pallas_call(
        _project_kernel,
        grid_spec=grid_spec,
        out_shape=[jax.ShapeDtypeStruct((nbl, h, modes), jnp.float32)] * 2,
        compiler_params=pltpu.CompilerParams(
            dimension_semantics=("arbitrary",),
            vmem_limit_bytes=56 * 1024 * 1024,
        ),
    )(rows, cols, side, pt, stiffness)


def _dft_kernel(w_ref, x_ref, own_ref, far_ref):
    x = x_ref[...]
    xh = x.astype(jnp.bfloat16)
    xl = (x - xh.astype(jnp.float32)).astype(jnp.bfloat16)
    w = w_ref[...]
    wh = w.astype(jnp.bfloat16)
    wl = (w - wh.astype(jnp.float32)).astype(jnp.bfloat16)
    acc = jnp.dot(wh, xh, preferred_element_type=jnp.float32)
    acc += jnp.dot(wh, xl, preferred_element_type=jnp.float32)
    acc += jnp.dot(wl, xh, preferred_element_type=jnp.float32)
    k = own_ref.shape[0]
    own_ref[...] = acc[:k]
    far_ref[...] = acc[k:].astype(far_ref.dtype)


def _dft(weights, x, own):
    rows, k = weights.shape
    n = x.shape[1]
    tn = 8192 if n % 8192 == 0 else n
    return pl.pallas_call(
        _dft_kernel,
        grid=(n // tn,),
        in_specs=[
            pl.BlockSpec((rows, k), lambda i: (0, 0)),
            pl.BlockSpec((k, tn), lambda i: (0, i)),
        ],
        out_specs=[
            pl.BlockSpec((own, tn), lambda i: (0, i)),
            pl.BlockSpec((rows - own, tn), lambda i: (0, i)),
        ],
        out_shape=[
            jax.ShapeDtypeStruct((own, n), jnp.float32),
            jax.ShapeDtypeStruct((rows - own, n), jnp.bfloat16),
        ],
        compiler_params=pltpu.CompilerParams(dimension_semantics=("arbitrary",)),
    )(weights, x)


def _trig(h, b, count):
    angle = ((h * b) % count).astype(jnp.float32) * (2.0 * math.pi / count)
    return jnp.cos(angle), -jnp.sin(angle)


def body(panel, stiffness, block_rows, block_cols):
    nbl, nblk, bs, _ = stiffness.shape
    modes = panel.shape[-1]
    nbd = lax.axis_size("blade")
    mine = jnp.swapaxes(panel.reshape(-1, bs, modes), 1, 2)
    pt = lax.all_gather(mine, ("blade", "dof"), axis=0, tiled=True)
    nd = lax.axis_size("dof")
    side = (lax.axis_index("dof") % 2).reshape(1).astype(jnp.int32)
    mine, other = _project(pt, stiffness, block_rows.reshape(-1), block_cols.reshape(-1), side)

    if nd == 2:
        half = mine + lax.ppermute(other, "dof", [(0, 1), (1, 0)])
    else:
        proj = jnp.concatenate([mine, other], axis=1)
        half = lax.psum_scatter(proj, "dof", scatter_dimension=1, tiled=True)
    me = lax.axis_index("blade")
    rows_half = half.shape[1]
    r = rows_half // nbd
    chunks = half.reshape(nbl, nbd, r, modes)

    got = []
    for s in range(nbd):
        piece = lax.dynamic_index_in_dim(chunks, (me + s) % nbd, axis=1, keepdims=False)
        if s:
            piece = lax.ppermute(piece, "blade", [(j, (j + s) % nbd) for j in range(nbd)])
        got.append(piece)
    stacked = jnp.stack(got).reshape(nbd * nbl, r * modes)

    count = nbl * nbd
    src = (me - jnp.arange(nbd, dtype=jnp.int32)) % nbd
    blade = (nbl * src[:, None] + jnp.arange(nbl, dtype=jnp.int32)[None, :]).reshape(-1)
    dst = (me + jnp.arange(nbd, dtype=jnp.int32)) % nbd
    harm = (nbl * dst[:, None] + jnp.arange(nbl, dtype=jnp.int32)[None, :]).reshape(-1)
    cosine, sine = _trig(harm[:, None], blade[None, :], count)
    weights = jnp.stack([cosine.reshape(nbd, nbl, -1), sine.reshape(nbd, nbl, -1)], axis=1)
    own, far = _dft(weights.reshape(2 * count, count), stacked, 2 * nbl)
    far = far.reshape(nbd - 1, 2, nbl, r, modes)

    out = jnp.zeros((2, nbl, rows_half, modes), jnp.float32)
    for t in range(nbd):
        if t:
            piece = far[t - 1]
            piece = lax.ppermute(piece, "blade", [(j, (j + t) % nbd) for j in range(nbd)])
            piece = piece.astype(jnp.float32)
        else:
            piece = own.reshape(2, nbl, r, modes)
        at = ((me - t) % nbd) * r
        out = lax.dynamic_update_slice(out, piece, (0, 0, at, 0))
    return out


def solution(mesh):
    placed = (
        P(("grp", "blade", "dof"), None),
        P(("grp", "blade"), "dof", None, None),
        P(("grp", "blade"), "dof"),
        P(("grp", "blade"), "dof"),
    )
    return jax.shard_map(
        body,
        mesh=mesh,
        in_specs=placed,
        out_specs=P(None, ("grp", "blade"), "dof", None),
        check_vma=False,
    )
```
